32 devices in a mesh: groups: 2 (over y), space: 4 (over z), blk: 2 (over x), samp: 2 (over core).
Axes of the slice: x: 2, y: 2, z: 4, core: 2. Of those that a mesh axis runs over, the one named last changes fastest.
Arguments:
- coeff: bfloat16 [16, 4, 512, 512], P(('groups', 'space', 'blk')), parts along dimension 0, may hold values from -0.125 to 0.125
- solve: bfloat16 [16, 512, 512], P(('groups', 'space', 'blk')), parts along dimension 0
- noise: float32 [16, 512, 512], P(('groups', 'space', 'blk'), 'samp'), parts along dimension 0, may hold values from -6 to 6
- prior: bfloat16 [16, 512, 512], P(('groups', 'space', 'blk'), 'samp'), parts along dimension 0, may hold values from -6 to 6
- owner: int32 [16], P('groups'), parts along dimension 0, may hold values from 0 to 7, as said below
- nbrs: int32 [16, 4], P('groups'), parts along dimension 0, may hold values from 0 to 15, as said below
Outputs:
- field: bfloat16 [16, 512, 512], P(('groups', 'space', 'blk'), 'samp'), parts along dimension 0
The draws below stay inside these ranges and needn't reach their ends.
There are 2 independent parts, one for each index of `groups`. The reference program is written for one: setup_inputs(seed, part) draws one part's arguments, and reference() takes and returns one part's arrays. A program takes and returns all parts, laid end to end along the dimension named above; each array names one. Nothing has to cross between parts.
Inputs may be any that keep to these rules, and one draw needn't show every extreme that they name: `owner`: A permutation of the blocks. `nbrs`: the 4 entries of a block are distinct. An entry v < 8 names block v's prior field; v >= 8 names the field of block v - 8; these references form no cycle, and every chain of them holds at most 4 blocks. The slot of every named block lies in a partition (slot // 2) at most 1 away from the reader's partition.
All inputs are finite; a program needn't handle non-finite values.
Results may differ from the reference program's by a relative error of at most 0.0056.
Values may be sent and summed in bfloat16 or wider, within the bound.
No kernel may reach another device: no remote copies, remote signals or barrier semaphores. Data moves between devices by JAX's collectives and lax.ppermute only.
A program may use at most 64 MiB of HBM per device.

```python
import jax
import jax.numpy as jnp
from jax import lax

B = 512
NEIGH = 4
LEVELS = 4
REACH = 1
SAMPLES = 512
PART = 2
NB = 8


def layout_tables(key):
    count = NB
    block_ids = jnp.arange(count, dtype=jnp.int32)
    owner = jax.random.permutation(jax.random.fold_in(key, 11), count).astype(jnp.int32)
    first_slot = owner[0]
    partner = jnp.bitwise_xor(first_slot, 1).astype(jnp.int32)
    holder = jnp.sum(jnp.where(owner == partner, block_ids, 0)).astype(jnp.int32)
    owner = owner.at[holder].set(owner[count - 1]).at[count - 1].set(partner)
    slot_level = jax.random.randint(jax.random.fold_in(key, 12), (count,), 0, LEVELS).astype(jnp.int32)
    slot_level = slot_level.at[first_slot].set(LEVELS - 1).at[partner].set(0)
    block_at = jnp.zeros((count,), jnp.int32).at[owner].set(block_ids)
    candidate = jnp.arange(2 * count, dtype=jnp.int32)
    cand_slot = jnp.remainder(candidate, count)
    cand_kind = candidate // count
    reader_part = block_ids // PART
    cand_part = cand_slot // PART
    nearby = jnp.abs(cand_part[None, :] - reader_part[:, None]) <= REACH
    earlier = (cand_kind[None, :] == 0) | (slot_level[cand_slot][None, :] < slot_level[:, None])
    scores = jax.random.randint(jax.random.fold_in(key, 13), (count, 2 * count), 0, 65536).astype(jnp.int32) * (2 * count) + candidate[None, :]
    scores = scores.at[first_slot, first_slot].set(1073741822).at[first_slot, count + partner].set(1073741823)
    scores = jnp.where(nearby & earlier, scores, -1 - candidate[None, :])
    chosen = lax.top_k(scores, NEIGH)[1].astype(jnp.int32)
    listed = chosen // count * count + block_at[jnp.remainder(chosen, count)]
    return (owner, listed[owner])


def draw_owner(key, part):
    return layout_tables(key)[0]


def draw_nbrs(key, part):
    return layout_tables(key)[1]


def draw_solve(key, part):
    shape = (NB, B, B)
    row_idx = lax.broadcasted_iota(jnp.int32, shape, 1)
    col_idx = lax.broadcasted_iota(jnp.int32, shape, 2)
    upper = jax.random.normal(jax.random.fold_in(key, 21), shape, jnp.float32) * (0.5 / jnp.sqrt(1.0 * B))
    diag = jnp.exp(jax.random.uniform(jax.random.fold_in(key, 22), shape, jnp.float32, -0.6931, 0.6931))
    matrix = jnp.where(row_idx < col_idx, upper, jnp.where(row_idx == col_idx, diag, 0.0))
    return matrix.astype(jnp.bfloat16)


def level_of(key, dims, pieces, smallest, high):
    factor_of = 1.0
    for dim, shards_of in pieces:
        steps = jax.random.uniform(jax.random.fold_in(jax.random.fold_in(key, 6), dim), (shards_of,), jnp.float32, smallest / len(pieces), high / len(pieces))
        factor_of = factor_of * jnp.repeat(jnp.exp(steps), dims[dim] // shards_of).reshape((-1,) + (1,) * (len(dims) - 1 - dim))
    return factor_of


def centred(stream_key, shape, scale, most, shards=(), kind=jnp.bfloat16):
    values = scale * jax.random.normal(stream_key, shape, jnp.float32)
    if shards:
        values = values * level_of(stream_key, shape, shards, -0.22, 0.18)
    return jnp.clip(values, -most, most).astype(kind)


def setup_inputs(seed: int = 0, part: int = 0) -> dict:
    streams_of = jax.random.split(jax.random.key(seed), 7)
    part_keys = jax.random.split(jax.random.fold_in(streams_of[6], part), 7)
    coeff = centred(part_keys[0], (NB, NEIGH, B, B), (NEIGH * B) ** -0.5, 0.125, ((0, 8),))
    solve = draw_solve(jax.random.fold_in(jax.random.fold_in(streams_of[6], part), 71), part)
    noise = centred(part_keys[2], (NB, SAMPLES, B), 1.0, 6.0, ((0, 8), (1, 2)), jnp.float32)
    prior = centred(part_keys[3], (NB, SAMPLES, B), 1.0, 6.0, ((0, 8), (1, 2)))
    owner = draw_owner(jax.random.fold_in(jax.random.fold_in(streams_of[6], part), 71), part)
    nbrs = draw_nbrs(jax.random.fold_in(jax.random.fold_in(streams_of[6], part), 71), part)
    return {"coeff": coeff, "solve": solve, "noise": noise, "prior": prior, "owner": owner, "nbrs": nbrs}


def block_levels(nbrs, count):
    is_current = nbrs >= count
    target = jnp.remainder(nbrs, count).astype(jnp.int32)
    levels = jnp.zeros((count,), jnp.int32)
    for sweep in range(LEVELS):
        above = jnp.where(is_current, levels[target] + 1, 0)
        levels = jnp.max(above, axis=1).astype(jnp.int32)
    return levels


def reference(coeff, solve, noise, prior, owner, nbrs):
    count = owner.shape[0]
    block_ids = jnp.arange(count, dtype=jnp.int32)
    block_at = jnp.zeros((count,), jnp.int32).at[owner].set(block_ids)
    level = block_levels(nbrs, count)
    slot_level = level[block_at]
    ordering = jnp.argsort(slot_level, stable=True).astype(jnp.int32)

    def advance(field, own_slot):
        own_block = block_at[own_slot]
        listed = nbrs[own_block]
        near_slot = owner[jnp.remainder(listed, count)].astype(jnp.int32)
        is_current = listed >= count
        values = jnp.where(is_current[:, None, None], field[near_slot], prior[near_slot]).astype(jnp.float32)
        mixed = jnp.einsum("jsq,jqp->sp", values, coeff[own_slot].astype(jnp.float32))
        right_side = (noise[own_slot] - mixed).astype(jnp.bfloat16)
        result = jnp.dot(right_side, solve[own_slot], preferred_element_type=jnp.float32).astype(jnp.bfloat16)
        return field.at[own_slot].set(result.astype(field.dtype)), None

    start = jnp.zeros(prior.shape, jnp.bfloat16).astype(prior.dtype)
    field, unused = lax.scan(advance, start, ordering)
    return field
```

```python
import jax
import jax.numpy as jnp
from jax import lax
from jax.sharding import PartitionSpec as P

LEVELS = 4
REACH = 1


def block_levels(nbrs, count):
    block_ids = jnp.arange(count, dtype=jnp.int32)
    is_current = nbrs >= count
    target = jnp.remainder(nbrs, count)
    picks = target[:, :, None] == block_ids[None, None, :]
    levels = jnp.zeros((count,), jnp.int32)
    for sweep in range(LEVELS):
        looked = jnp.sum(jnp.where(picks, levels[None, None, :], 0), axis=2)
        above = jnp.where(is_current, looked + 1, 0)
        levels = jnp.max(above, axis=1)
    return levels


def window_pairs(space_count, part_size, distance, offset):
    pairs = []
    for space_to in range(space_count):
        space_from = space_to + distance
        if not 0 <= space_from < space_count:
            continue
        for blk_to in range(part_size):
            blk_from = (blk_to + offset) % part_size
            pairs.append((space_from * part_size + blk_from, space_to * part_size + blk_to))
    return pairs


def neighbourhood(local_block):
    part_size = lax.axis_size("blk")
    space_count = lax.axis_size("space")
    pieces = []
    for distance in range(-REACH, REACH + 1):
        for offset in range(part_size):
            if distance == 0 and offset == 0:
                pieces.append(local_block)
                continue
            pairs = window_pairs(space_count, part_size, distance, offset)
            pieces.append(lax.ppermute(local_block, ("space", "blk"), pairs))
    return jnp.stack(pieces, axis=0)


def body(coeff, solve, noise, prior, owner, nbrs):
    part_size = lax.axis_size("blk")
    space_index = lax.axis_index("space")
    blk_index = lax.axis_index("blk")
    own_slot = space_index * part_size + blk_index
    count = owner.shape[0]
    neigh = nbrs.shape[1]
    block_ids = jnp.arange(count, dtype=jnp.int32)
    levels = block_levels(nbrs, count)
    own_block = jnp.sum(jnp.where(owner == own_slot, block_ids, 0))
    own_level = jnp.sum(jnp.where(block_ids == own_block, levels, 0))
    own_list = jnp.sum(jnp.where((block_ids == own_block)[:, None], nbrs, 0), axis=0)
    is_current = own_list >= count
    target = jnp.remainder(own_list, count)
    near_slot = jnp.sum(jnp.where(target[:, None] == block_ids[None, :], owner[None, :], 0), axis=1)
    distance = near_slot // part_size - space_index
    offset = jnp.remainder(near_slot - blk_index, part_size)
    piece = (distance + REACH) * part_size + offset

    prior_window = neighbourhood(prior[0])
    start = noise[0]
    for j in range(neigh):
        values = lax.dynamic_index_in_dim(prior_window, piece[j], 0, keepdims=False)
        term = jnp.dot(values, coeff[0, j], preferred_element_type=jnp.float32)
        start = start - jnp.where(is_current[j], jnp.zeros_like(term), term)

    current = jnp.zeros_like(prior[0])
    window = None
    for level_now in range(LEVELS):

        def compute_block(previous, window_now=window):
            right_side = start
            if window_now is not None:
                for j in range(neigh):
                    values = lax.dynamic_index_in_dim(window_now, piece[j], 0, keepdims=False)
                    term = jnp.dot(values, coeff[0, j], preferred_element_type=jnp.float32)
                    right_side = right_side - jnp.where(is_current[j], term, jnp.zeros_like(term))
            result = jnp.dot(right_side.astype(jnp.bfloat16), solve[0], preferred_element_type=jnp.float32)
            return result.astype(jnp.bfloat16)

        def unchanged(previous):
            return previous

        current = lax.cond(own_level == level_now, compute_block, unchanged, current)
        if level_now + 1 < LEVELS:
            window = neighbourhood(current)
    return current[None]


def solution(mesh):
    placed = (
        P(("groups", "space", "blk"), None, None, None),
        P(("groups", "space", "blk"), None, None),
        P(("groups", "space", "blk"), "samp", None),
        P(("groups", "space", "blk"), "samp", None),
        P("groups"),
        P("groups", None),
    )
    return jax.shard_map(
        body,
        mesh=mesh,
        in_specs=placed,
        out_specs=P(("groups", "space", "blk"), "samp", None),
        check_vma=False,
    )
```

```python
import functools

import jax
import jax.numpy as jnp
from jax import lax
from jax.experimental import pallas as pl
from jax.experimental.pallas import tpu as pltpu
from jax.sharding import PartitionSpec as P

LEVELS = 4
REACH = 1


def block_levels(nbrs, count):
    block_ids = jnp.arange(count, dtype=jnp.int32)
    is_current = nbrs >= count
    target = jnp.remainder(nbrs, count)
    picks = target[:, :, None] == block_ids[None, None, :]
    levels = jnp.zeros((count,), jnp.int32)
    for sweep in range(LEVELS):
        looked = jnp.sum(jnp.where(picks, levels[None, None, :], 0), axis=2)
        above = jnp.where(is_current, looked + 1, 0)
        levels = jnp.max(above, axis=1)
    return levels


def window_pairs(space_count, part_size, distance, offset):
    pairs = []
    for space_to in range(space_count):
        space_from = space_to + distance
        if not 0 <= space_from < space_count:
            continue
        for blk_to in range(part_size):
            blk_from = (blk_to + offset) % part_size
            pairs.append((space_from * part_size + blk_from, space_to * part_size + blk_to))
    return pairs


def neighbourhood(local_block):
    part_size = lax.axis_size("blk")
    space_count = lax.axis_size("space")
    pieces = []
    for distance in range(-REACH, REACH + 1):
        for offset in range(part_size):
            if distance == 0 and offset == 0:
                pieces.append(local_block)
                continue
            pairs = window_pairs(space_count, part_size, distance, offset)
            pieces.append(lax.ppermute(local_block, ("space", "blk"), pairs))
    return pieces


def mix_kernel(n_pieces, neigh, finish, pick_ref, use_ref, start_ref, coeff_ref, *rest):
    if finish:
        solve_ref, rest = rest[0], rest[1:]
    pieces = rest[:n_pieces]
    out_ref, values, acc, sems = rest[n_pieces:]
    for j in range(neigh):
        for p in range(n_pieces):

            @pl.when((pick_ref[j] == p) & (use_ref[j] != 0))
            def _():
                pltpu.make_async_copy(pieces[p], values.at[j], sems.at[j]).start()

    acc[...] = start_ref[...]
    for j in range(neigh):

        @pl.when(use_ref[j] != 0)
        def _():
            pltpu.make_async_copy(pieces[0], values.at[j], sems.at[j]).wait()
            acc[...] -= jnp.dot(values[j], coeff_ref[j], preferred_element_type=jnp.float32)

    if finish:
        right_side = acc[...].astype(jnp.bfloat16)
        out_ref[...] = jnp.dot(right_side, solve_ref[...], preferred_element_type=jnp.float32).astype(out_ref.dtype)
    else:
        out_ref[...] = acc[...]


def mix(pick, use, start, coeff, pieces, solve=None):
    neigh = coeff.shape[0]
    rows, cols = start.shape
    finish = solve is not None
    vmem = pl.BlockSpec(memory_space=pltpu.VMEM)
    smem = pl.BlockSpec(memory_space=pltpu.SMEM)
    anywhere = pl.BlockSpec(memory_space=pl.ANY)
    operands = [pick, use, start, coeff] + ([solve] if finish else []) + list(pieces)
    in_specs = [smem, smem, vmem, vmem] + ([vmem] if finish else []) + [anywhere] * len(pieces)
    out_dtype = jnp.bfloat16 if finish else jnp.float32
    flops = 2 * rows * cols * coeff.shape[1] * (neigh + (1 if finish else 0))
    return pl.pallas_call(
        functools.partial(mix_kernel, len(pieces), neigh, finish),
        out_shape=jax.ShapeDtypeStruct((rows, cols), out_dtype),
        in_specs=in_specs,
        out_specs=vmem,
        scratch_shapes=[
            pltpu.VMEM((neigh, rows, coeff.shape[1]), pieces[0].dtype),
            pltpu.VMEM((rows, cols), jnp.float32),
            pltpu.SemaphoreType.DMA((neigh,)),
        ],
        cost_estimate=pl.CostEstimate(
            flops=flops, bytes_accessed=2 * (neigh + 1) * rows * cols * 4 + coeff.size * 2, transcendentals=0
        ),
    )(*operands)


def body(coeff, solve, noise, prior, owner, nbrs):
    part_size = lax.axis_size("blk")
    space_index = lax.axis_index("space")
    blk_index = lax.axis_index("blk")
    own_slot = space_index * part_size + blk_index
    count = owner.shape[0]
    block_ids = jnp.arange(count, dtype=jnp.int32)
    levels = block_levels(nbrs, count)
    own_block = jnp.sum(jnp.where(owner == own_slot, block_ids, 0))
    own_level = jnp.sum(jnp.where(block_ids == own_block, levels, 0))
    own_list = jnp.sum(jnp.where((block_ids == own_block)[:, None], nbrs, 0), axis=0)
    is_current = (own_list >= count).astype(jnp.int32)
    target = jnp.remainder(own_list, count)
    near_slot = jnp.sum(jnp.where(target[:, None] == block_ids[None, :], owner[None, :], 0), axis=1)
    distance = near_slot // part_size - space_index
    offset = jnp.remainder(near_slot - blk_index, part_size)
    pick = ((distance + REACH) * part_size + offset).astype(jnp.int32)

    prior_pieces = neighbourhood(prior[0])
    start = mix(pick, 1 - is_current, noise[0], coeff[0], prior_pieces)

    current = jnp.zeros_like(prior[0])
    pieces = None
    for level_now in range(LEVELS):

        def compute_block(previous, pieces_now=pieces):
            if pieces_now is None:
                right_side = start.astype(jnp.bfloat16)
                result = jnp.dot(right_side, solve[0], preferred_element_type=jnp.float32)
                return result.astype(jnp.bfloat16)
            return mix(pick, is_current, start, coeff[0], pieces_now, solve[0])

        def unchanged(previous):
            return previous

        current = lax.cond(own_level == level_now, compute_block, unchanged, current)
        if level_now + 1 < LEVELS:
            pieces = neighbourhood(current)
    return current[None]


def solution(mesh):
    placed = (
        P(("groups", "space", "blk"), None, None, None),
        P(("groups", "space", "blk"), None, None),
        P(("groups", "space", "blk"), "samp", None),
        P(("groups", "space", "blk"), "samp", None),
        P("groups"),
        P("groups", None),
    )
    return jax.shard_map(
        body,
        mesh=mesh,
        in_specs=placed,
        out_specs=P(("groups", "space", "blk"), "samp", None),
        check_vma=False,
    )
```

```python
import functools

import jax
import jax.numpy as jnp
from jax import lax
from jax.experimental import pallas as pl
from jax.experimental.pallas import tpu as pltpu
from jax.sharding import PartitionSpec as P

LEVELS = 4
REACH = 1


def block_levels(nbrs, count):
    block_ids = jnp.arange(count, dtype=jnp.int32)
    is_current = nbrs >= count
    target = jnp.remainder(nbrs, count)
    picks = target[:, :, None] == block_ids[None, None, :]
    levels = jnp.zeros((count,), jnp.int32)
    for sweep in range(LEVELS):
        looked = jnp.sum(jnp.where(picks, levels[None, None, :], 0), axis=2)
        above = jnp.where(is_current, looked + 1, 0)
        levels = jnp.max(above, axis=1)
    return levels


def window_pairs(space_count, part_size, distance, offset):
    pairs = []
    for space_to in range(space_count):
        space_from = space_to + distance
        if not 0 <= space_from < space_count:
            continue
        for blk_to in range(part_size):
            blk_from = (blk_to + offset) % part_size
            pairs.append((space_from * part_size + blk_from, space_to * part_size + blk_to))
    return pairs


def neighbourhood(local_block):
    part_size = lax.axis_size("blk")
    space_count = lax.axis_size("space")
    pieces = []
    for distance in range(-REACH, REACH + 1):
        for offset in range(part_size):
            if distance == 0 and offset == 0:
                pieces.append(local_block)
                continue
            pairs = window_pairs(space_count, part_size, distance, offset)
            pieces.append(lax.ppermute(local_block, ("space", "blk"), pairs))
    return pieces


def mix_kernel(n_pieces, neigh, finish, pick_ref, use_ref, start_ref, coeff_ref, *rest):
    if finish:
        solve_ref, rest = rest[0], rest[1:]
    pieces = rest[:n_pieces]
    out_ref, values, acc, sems = rest[n_pieces:]
    for j in range(neigh):
        for p in range(n_pieces):

            @pl.when((pick_ref[j] == p) & (use_ref[j] != 0))
            def _():
                pltpu.make_async_copy(pieces[p], values.at[j], sems.at[j]).start()

    acc[...] = start_ref[...]
    for j in range(neigh):

        @pl.when(use_ref[j] != 0)
        def _():
            pltpu.make_async_copy(pieces[0], values.at[j], sems.at[j]).wait()
            acc[...] -= jnp.dot(values[j], coeff_ref[j], preferred_element_type=jnp.float32)

    if finish:
        right_side = acc[...].astype(jnp.bfloat16)
        out_ref[...] = jnp.dot(right_side, solve_ref[...], preferred_element_type=jnp.float32).astype(out_ref.dtype)
    else:
        out_ref[...] = acc[...]


def mix(pick, use, start, coeff, pieces, solve=None):
    neigh = coeff.shape[0]
    rows, cols = start.shape
    finish = solve is not None
    vmem = pl.BlockSpec(memory_space=pltpu.VMEM)
    smem = pl.BlockSpec(memory_space=pltpu.SMEM)
    anywhere = pl.BlockSpec(memory_space=pl.ANY)
    operands = [pick, use, start, coeff] + ([solve] if finish else []) + list(pieces)
    in_specs = [smem, smem, vmem, vmem] + ([vmem] if finish else []) + [anywhere] * len(pieces)
    out_dtype = jnp.bfloat16 if finish else jnp.float32
    flops = 2 * rows * cols * coeff.shape[1] * (neigh + (1 if finish else 0))
    return pl.pallas_call(
        functools.partial(mix_kernel, len(pieces), neigh, finish),
        out_shape=jax.ShapeDtypeStruct((rows, cols), out_dtype),
        in_specs=in_specs,
        out_specs=vmem,
        scratch_shapes=[
            pltpu.VMEM((neigh, rows, coeff.shape[1]), pieces[0].dtype),
            pltpu.VMEM((rows, cols), jnp.float32),
            pltpu.SemaphoreType.DMA((neigh,)),
        ],
        cost_estimate=pl.CostEstimate(
            flops=flops, bytes_accessed=2 * (neigh + 1) * rows * cols * 4 + coeff.size * 2, transcendentals=0
        ),
    )(*operands)


def body(coeff, solve, noise, prior, owner, nbrs):
    part_size = lax.axis_size("blk")
    space_index = lax.axis_index("space")
    blk_index = lax.axis_index("blk")
    own_slot = space_index * part_size + blk_index
    count = owner.shape[0]
    block_ids = jnp.arange(count, dtype=jnp.int32)
    levels = block_levels(nbrs, count)
    own_block = jnp.sum(jnp.where(owner == own_slot, block_ids, 0))
    own_level = jnp.sum(jnp.where(block_ids == own_block, levels, 0))
    own_list = jnp.sum(jnp.where((block_ids == own_block)[:, None], nbrs, 0), axis=0)
    is_current = (own_list >= count).astype(jnp.int32)
    target = jnp.remainder(own_list, count)
    near_slot = jnp.sum(jnp.where(target[:, None] == block_ids[None, :], owner[None, :], 0), axis=1)
    distance = near_slot // part_size - space_index
    offset = jnp.remainder(near_slot - blk_index, part_size)
    pick = ((distance + REACH) * part_size + offset).astype(jnp.int32)

    prior_pieces = neighbourhood(prior[0])
    start = mix(pick, 1 - is_current, noise[0], coeff[0], prior_pieces)

    deepest = lax.pmax(jnp.max(levels), "groups")

    current = jnp.zeros_like(prior[0])
    pieces = None
    for level_now in range(LEVELS):

        def compute_block(previous, pieces_now=pieces):
            if pieces_now is None:
                right_side = start.astype(jnp.bfloat16)
                result = jnp.dot(right_side, solve[0], preferred_element_type=jnp.float32)
                return result.astype(jnp.bfloat16)
            return mix(pick, is_current, start, coeff[0], pieces_now, solve[0])

        def unchanged(previous):
            return previous

        current = lax.cond(own_level == level_now, compute_block, unchanged, current)
        if level_now + 1 < LEVELS:
            pieces = lax.cond(
                deepest > level_now,
                lambda block: tuple(neighbourhood(block)),
                lambda block: tuple(jnp.zeros_like(block) for _ in prior_pieces),
                current,
            )
    return current[None]


def solution(mesh):
    placed = (
        P(("groups", "space", "blk"), None, None, None),
        P(("groups", "space", "blk"), None, None),
        P(("groups", "space", "blk"), "samp", None),
        P(("groups", "space", "blk"), "samp", None),
        P("groups"),
        P("groups", None),
    )
    return jax.shard_map(
        body,
        mesh=mesh,
        in_specs=placed,
        out_specs=P(("groups", "space", "blk"), "samp", None),
        check_vma=False,
    )
```

```python
import functools

import jax
import jax.numpy as jnp
from jax import lax
from jax.experimental import pallas as pl
from jax.experimental.pallas import tpu as pltpu
from jax.sharding import PartitionSpec as P

LEVELS = 4
REACH = 1


def block_levels(nbrs, count):
    block_ids = jnp.arange(count, dtype=jnp.int32)
    is_current = nbrs >= count
    target = jnp.remainder(nbrs, count)
    picks = target[:, :, None] == block_ids[None, None, :]
    levels = jnp.zeros((count,), jnp.int32)
    for sweep in range(LEVELS):
        looked = jnp.sum(jnp.where(picks, levels[None, None, :], 0), axis=2)
        above = jnp.where(is_current, looked + 1, 0)
        levels = jnp.max(above, axis=1)
    return levels


def window_pairs(space_count, part_size, distance, offset):
    pairs = []
    for space_to in range(space_count):
        space_from = space_to + distance
        if not 0 <= space_from < space_count:
            continue
        for blk_to in range(part_size):
            blk_from = (blk_to + offset) % part_size
            pairs.append((space_from * part_size + blk_from, space_to * part_size + blk_to))
    return pairs


def neighbourhood(local_block):
    part_size = lax.axis_size("blk")
    space_count = lax.axis_size("space")
    pieces = []
    for distance in range(-REACH, REACH + 1):
        for offset in range(part_size):
            if distance == 0 and offset == 0:
                pieces.append(local_block)
                continue
            pairs = window_pairs(space_count, part_size, distance, offset)
            pieces.append(lax.ppermute(local_block, ("space", "blk"), pairs))
    return pieces


def mix_kernel(n_pieces, neigh, finish, pick_ref, use_ref, start_ref, coeff_ref, *rest):
    if finish:
        solve_ref, rest = rest[0], rest[1:]
    pieces = rest[:n_pieces]
    out_ref, values, acc, sems = rest[n_pieces:]
    for j in range(neigh):
        for p in range(n_pieces):

            @pl.when((pick_ref[j] == p) & (use_ref[j] != 0))
            def _():
                pltpu.make_async_copy(pieces[p], values.at[j], sems.at[j]).start()

    acc[...] = start_ref[...]
    for j in range(neigh):

        @pl.when(use_ref[j] != 0)
        def _():
            pltpu.make_async_copy(pieces[0], values.at[j], sems.at[j]).wait()
            acc[...] -= jnp.dot(values[j], coeff_ref[j], preferred_element_type=jnp.float32)

    if finish:
        right_side = acc[...].astype(jnp.bfloat16)
        out_ref[...] = jnp.dot(right_side, solve_ref[...], preferred_element_type=jnp.float32).astype(out_ref.dtype)
    else:
        out_ref[...] = acc[...]


def mix(pick, use, start, coeff, pieces, solve=None):
    neigh = coeff.shape[0]
    rows, cols = start.shape
    finish = solve is not None
    vmem = pl.BlockSpec(memory_space=pltpu.VMEM)
    smem = pl.BlockSpec(memory_space=pltpu.SMEM)
    anywhere = pl.BlockSpec(memory_space=pl.ANY)
    operands = [pick, use, start, coeff] + ([solve] if finish else []) + list(pieces)
    in_specs = [smem, smem, vmem, vmem] + ([vmem] if finish else []) + [anywhere] * len(pieces)
    out_dtype = jnp.bfloat16 if finish else jnp.float32
    flops = 2 * rows * cols * coeff.shape[1] * (neigh + (1 if finish else 0))
    return pl.pallas_call(
        functools.partial(mix_kernel, len(pieces), neigh, finish),
        out_shape=jax.ShapeDtypeStruct((rows, cols), out_dtype),
        in_specs=in_specs,
        out_specs=vmem,
        scratch_shapes=[
            pltpu.VMEM((neigh, rows, coeff.shape[1]), pieces[0].dtype),
            pltpu.VMEM((rows, cols), jnp.float32),
            pltpu.SemaphoreType.DMA((neigh,)),
        ],
        cost_estimate=pl.CostEstimate(
            flops=flops, bytes_accessed=2 * (neigh + 1) * rows * cols * 4 + coeff.size * 2, transcendentals=0
        ),
    )(*operands)


def body(coeff, solve, noise, prior, owner, nbrs):
    part_size = lax.axis_size("blk")
    space_index = lax.axis_index("space")
    blk_index = lax.axis_index("blk")
    own_slot = space_index * part_size + blk_index
    count = owner.shape[0]
    block_ids = jnp.arange(count, dtype=jnp.int32)
    levels = block_levels(nbrs, count)
    own_block = jnp.sum(jnp.where(owner == own_slot, block_ids, 0))
    own_level = jnp.sum(jnp.where(block_ids == own_block, levels, 0))
    own_list = jnp.sum(jnp.where((block_ids == own_block)[:, None], nbrs, 0), axis=0)
    is_current = (own_list >= count).astype(jnp.int32)
    target = jnp.remainder(own_list, count)
    near_slot = jnp.sum(jnp.where(target[:, None] == block_ids[None, :], owner[None, :], 0), axis=1)
    distance = near_slot // part_size - space_index
    offset = jnp.remainder(near_slot - blk_index, part_size)
    pick = ((distance + REACH) * part_size + offset).astype(jnp.int32)

    prior_pieces = neighbourhood(prior[0])
    start = mix(pick, 1 - is_current, noise[0], coeff[0], prior_pieces)

    deepest = jnp.max(levels)
    if lax.axis_size("groups") == 2:
        deepest = jnp.maximum(deepest, lax.ppermute(deepest, "groups", [(0, 1), (1, 0)]))
    else:
        deepest = lax.pmax(deepest, "groups")

    def unchanged(previous):
        return previous

    def first_block(previous):
        right_side = start.astype(jnp.bfloat16)
        return jnp.dot(right_side, solve[0], preferred_element_type=jnp.float32).astype(jnp.bfloat16)

    current = lax.cond(own_level == 0, first_block, unchanged, jnp.zeros_like(prior[0]))
    for level_now in range(1, LEVELS):

        def level_step(previous, level_now=level_now):
            pieces = neighbourhood(previous)

            def compute_block(block):
                return mix(pick, is_current, start, coeff[0], pieces, solve[0])

            return lax.cond(own_level == level_now, compute_block, unchanged, previous)

        current = lax.cond(deepest >= level_now, level_step, unchanged, current)
    return current[None]


def solution(mesh):
    placed = (
        P(("groups", "space", "blk"), None, None, None),
        P(("groups", "space", "blk"), None, None),
        P(("groups", "space", "blk"), "samp", None),
        P(("groups", "space", "blk"), "samp", None),
        P("groups"),
        P("groups", None),
    )
    return jax.shard_map(
        body,
        mesh=mesh,
        in_specs=placed,
        out_specs=P(("groups", "space", "blk"), "samp", None),
        check_vma=False,
    )
```

```python
import functools

import jax
import jax.numpy as jnp
from jax import lax
from jax.experimental import pallas as pl
from jax.experimental.pallas import tpu as pltpu
from jax.sharding import PartitionSpec as P

LEVELS = 4
REACH = 1


def block_levels(nbrs, count):
    block_ids = jnp.arange(count, dtype=jnp.int32)
    is_current = nbrs >= count
    target = jnp.remainder(nbrs, count)
    picks = target[:, :, None] == block_ids[None, None, :]
    levels = jnp.zeros((count,), jnp.int32)
    for sweep in range(LEVELS):
        looked = jnp.sum(jnp.where(picks, levels[None, None, :], 0), axis=2)
        above = jnp.where(is_current, looked + 1, 0)
        levels = jnp.max(above, axis=1)
    return levels


def window_pairs(space_count, part_size, distance, offset):
    pairs = []
    for space_to in range(space_count):
        space_from = space_to + distance
        if not 0 <= space_from < space_count:
            continue
        for blk_to in range(part_size):
            blk_from = (blk_to + offset) % part_size
            pairs.append((space_from * part_size + blk_from, space_to * part_size + blk_to))
    return pairs


def neighbourhood(local_block):
    part_size = lax.axis_size("blk")
    space_count = lax.axis_size("space")
    pieces = []
    for distance in range(-REACH, REACH + 1):
        for offset in range(part_size):
            if distance == 0 and offset == 0:
                pieces.append(local_block)
                continue
            pairs = window_pairs(space_count, part_size, distance, offset)
            pieces.append(lax.ppermute(local_block, ("space", "blk"), pairs))
    return pieces


def mix_kernel(n_pieces, neigh, pick_ref, use_ref, start_ref, coeff_hbm, *rest):
    pieces = rest[:n_pieces]
    out_ref, values, weights, sems = rest[n_pieces:]
    for j in range(neigh):

        @pl.when(use_ref[j] != 0)
        def _():
            pltpu.make_async_copy(coeff_hbm.at[0, j], weights.at[j], sems.at[1, j]).start()

        for p in range(n_pieces):

            @pl.when((pick_ref[j] == p) & (use_ref[j] != 0))
            def _():
                pltpu.make_async_copy(pieces[p], values.at[j], sems.at[0, j]).start()

    out_ref[...] = start_ref[...]
    for j in range(neigh):

        @pl.when(use_ref[j] != 0)
        def _():
            pltpu.make_async_copy(pieces[0], values.at[j], sems.at[0, j]).wait()
            pltpu.make_async_copy(coeff_hbm.at[0, j], weights.at[j], sems.at[1, j]).wait()
            out_ref[...] -= jnp.dot(values[j], weights[j], preferred_element_type=jnp.float32)


def mix(pick, use, start, coeff, pieces):
    neigh = coeff.shape[1]
    rows, cols = start.shape
    vmem = pl.BlockSpec(memory_space=pltpu.VMEM)
    smem = pl.BlockSpec(memory_space=pltpu.SMEM)
    anywhere = pl.BlockSpec(memory_space=pl.ANY)
    return pl.pallas_call(
        functools.partial(mix_kernel, len(pieces), neigh),
        out_shape=jax.ShapeDtypeStruct((rows, cols), jnp.float32),
        in_specs=[smem, smem, vmem, anywhere] + [anywhere] * len(pieces),
        out_specs=vmem,
        scratch_shapes=[
            pltpu.VMEM((neigh, rows, coeff.shape[2]), pieces[0].dtype),
            pltpu.VMEM(coeff.shape[1:], coeff.dtype),
            pltpu.SemaphoreType.DMA((2, neigh)),
        ],
        cost_estimate=pl.CostEstimate(
            flops=2 * rows * cols * coeff.shape[2] * neigh,
            bytes_accessed=(2 * neigh + 2) * rows * cols * 4 + coeff.size * 2,
            transcendentals=0,
        ),
    )(pick, use, start, coeff, *pieces)


def absorb_kernel(neigh, sel_ref, acc_ref, piece_ref, coeff_hbm, out_ref, weights, sems):
    for j in range(neigh):

        @pl.when(sel_ref[j] != 0)
        def _():
            pltpu.make_async_copy(coeff_hbm.at[0, j], weights.at[j], sems.at[j]).start()

    out_ref[...] = acc_ref[...]
    for j in range(neigh):

        @pl.when(sel_ref[j] != 0)
        def _():
            pltpu.make_async_copy(coeff_hbm.at[0, j], weights.at[j], sems.at[j]).wait()
            out_ref[...] -= jnp.dot(piece_ref[...], weights[j], preferred_element_type=jnp.float32)


def absorb(sel, acc, piece, coeff):
    neigh = coeff.shape[1]
    rows, cols = acc.shape
    vmem = pl.BlockSpec(memory_space=pltpu.VMEM)
    return pl.pallas_call(
        functools.partial(absorb_kernel, neigh),
        out_shape=jax.ShapeDtypeStruct((rows, cols), jnp.float32),
        in_specs=[pl.BlockSpec(memory_space=pltpu.SMEM), vmem, vmem, pl.BlockSpec(memory_space=pl.ANY)],
        out_specs=vmem,
        scratch_shapes=[
            pltpu.VMEM(coeff.shape[1:], coeff.dtype),
            pltpu.SemaphoreType.DMA((neigh,)),
        ],
        cost_estimate=pl.CostEstimate(
            flops=2 * rows * cols * coeff.shape[2], bytes_accessed=5 * rows * cols * 2 + coeff.size // neigh * 2, transcendentals=0
        ),
    )(sel, acc, piece, coeff)


def body(coeff, solve, noise, prior, owner, nbrs):
    part_size = lax.axis_size("blk")
    space_index = lax.axis_index("space")
    blk_index = lax.axis_index("blk")
    own_slot = space_index * part_size + blk_index
    count = owner.shape[0]
    block_ids = jnp.arange(count, dtype=jnp.int32)
    levels = block_levels(nbrs, count)
    own_block = jnp.sum(jnp.where(owner == own_slot, block_ids, 0))
    own_level = jnp.sum(jnp.where(block_ids == own_block, levels, 0))
    own_list = jnp.sum(jnp.where((block_ids == own_block)[:, None], nbrs, 0), axis=0)
    is_current = (own_list >= count).astype(jnp.int32)
    target = jnp.remainder(own_list, count)
    near_slot = jnp.sum(jnp.where(target[:, None] == block_ids[None, :], owner[None, :], 0), axis=1)
    distance = near_slot // part_size - space_index
    offset = jnp.remainder(near_slot - blk_index, part_size)
    pick = ((distance + REACH) * part_size + offset).astype(jnp.int32)

    arrives = jnp.where(is_current != 0, jnp.sum(jnp.where(target[:, None] == block_ids[None, :], levels[None, :], 0), axis=1) + 1, 0)
    width = (2 * REACH + 1) * part_size
    every_slot = owner[:, None]
    listed_slot = jnp.sum(jnp.where(jnp.remainder(nbrs, count)[:, :, None] == block_ids[None, None, :], owner[None, None, :], 0), axis=2)
    listed_piece = (listed_slot // part_size - every_slot // part_size + REACH) * part_size + jnp.remainder(
        listed_slot - every_slot, part_size
    )
    listed_level = jnp.sum(jnp.where(jnp.remainder(nbrs, count)[:, :, None] == block_ids[None, None, :], levels[None, None, :], 0), axis=2)
    listed_round = jnp.where(nbrs >= count, listed_level + 1, 0)
    rounds = jnp.arange(LEVELS, dtype=jnp.int32)
    piece_ids = jnp.arange(width, dtype=jnp.int32)
    hits = (listed_round[:, :, None, None] == rounds[:, None]) & (listed_piece[:, :, None, None] == piece_ids[None, :])
    need = jnp.max(jnp.where(hits, 1, 0), axis=(0, 1)).astype(jnp.int32)
    deepest = jnp.max(levels)
    if lax.axis_size("groups") == 2:
        deepest = jnp.maximum(deepest, lax.ppermute(deepest, "groups", [(0, 1), (1, 0)]))
        need = jnp.maximum(need, lax.ppermute(need, "groups", [(0, 1), (1, 0)]))
    else:
        deepest = lax.pmax(deepest, "groups")
        need = lax.pmax(need, "groups")

    prior_pieces = neighbourhood(prior[0])
    acc = mix(pick, 1 - is_current, noise[0], coeff, prior_pieces)

    def unchanged(previous):
        return previous

    def finished(block, total):
        right_side = total.astype(jnp.bfloat16)
        return jnp.dot(right_side, solve[0], preferred_element_type=jnp.float32).astype(jnp.bfloat16)

    current = lax.cond(own_level == 0, functools.partial(finished, total=acc), unchanged, jnp.zeros_like(prior[0]))
    for level_now in range(1, LEVELS):

        def level_step(carry, level_now=level_now):
            block, total = carry
            for distance in range(-REACH, REACH + 1):
                for offset in range(part_size):
                    if distance == 0 and offset == 0:
                        continue
                    index = (distance + REACH) * part_size + offset
                    sel = ((arrives == level_now) & (pick == index)).astype(jnp.int32)

                    def take(running, distance=distance, offset=offset, sel=sel):
                        pairs = window_pairs(lax.axis_size("space"), part_size, distance, offset)
                        piece = lax.ppermute(block, ("space", "blk"), pairs)
                        return absorb(sel, running, piece, coeff)

                    total = lax.cond(need[level_now, index] != 0, take, unchanged, total)
            block = lax.cond(own_level == level_now, functools.partial(finished, total=total), unchanged, block)
            return block, total

        current, acc = lax.cond(deepest >= level_now, level_step, unchanged, (current, acc))
    return current[None]


def solution(mesh):
    placed = (
        P(("groups", "space", "blk"), None, None, None),
        P(("groups", "space", "blk"), None, None),
        P(("groups", "space", "blk"), "samp", None),
        P(("groups", "space", "blk"), "samp", None),
        P("groups"),
        P("groups", None),
    )
    return jax.shard_map(
        body,
        mesh=mesh,
        in_specs=placed,
        out_specs=P(("groups", "space", "blk"), "samp", None),
        check_vma=False,
    )
```

```python
import functools

import jax
import jax.numpy as jnp
from jax import lax
from jax.experimental import pallas as pl
from jax.experimental.pallas import tpu as pltpu
from jax.sharding import PartitionSpec as P

LEVELS = 4
REACH = 1


def block_levels(nbrs, count):
    block_ids = jnp.arange(count, dtype=jnp.int32)
    is_current = nbrs >= count
    target = jnp.remainder(nbrs, count)
    picks = target[:, :, None] == block_ids[None, None, :]
    levels = jnp.zeros((count,), jnp.int32)
    for sweep in range(LEVELS):
        looked = jnp.sum(jnp.where(picks, levels[None, None, :], 0), axis=2)
        above = jnp.where(is_current, looked + 1, 0)
        levels = jnp.max(above, axis=1)
    return levels


def window_pairs(space_count, part_size, distance, offset):
    pairs = []
    for space_to in range(space_count):
        space_from = space_to + distance
        if not 0 <= space_from < space_count:
            continue
        for blk_to in range(part_size):
            blk_from = (blk_to + offset) % part_size
            pairs.append((space_from * part_size + blk_from, space_to * part_size + blk_to))
    return pairs


def neighbourhood(local_block):
    part_size = lax.axis_size("blk")
    space_count = lax.axis_size("space")
    pieces = []
    for distance in range(-REACH, REACH + 1):
        for offset in range(part_size):
            if distance == 0 and offset == 0:
                pieces.append(local_block)
                continue
            pairs = window_pairs(space_count, part_size, distance, offset)
            pieces.append(lax.ppermute(local_block, ("space", "blk"), pairs))
    return pieces


def mix_kernel(n_pieces, neigh, pick_ref, use_ref, start_ref, coeff_hbm, *rest):
    pieces = rest[:n_pieces]
    out_ref, values, weights, sems = rest[n_pieces:]
    for j in range(neigh):

        @pl.when(use_ref[j] != 0)
        def _():
            pltpu.make_async_copy(coeff_hbm.at[0, j], weights.at[j], sems.at[1, j]).start()

        for p in range(n_pieces):

            @pl.when((pick_ref[j] == p) & (use_ref[j] != 0))
            def _():
                pltpu.make_async_copy(pieces[p], values.at[j], sems.at[0, j]).start()

    out_ref[...] = start_ref[...]
    for j in range(neigh):

        @pl.when(use_ref[j] != 0)
        def _():
            pltpu.make_async_copy(pieces[0], values.at[j], sems.at[0, j]).wait()
            pltpu.make_async_copy(coeff_hbm.at[0, j], weights.at[j], sems.at[1, j]).wait()
            out_ref[...] -= jnp.dot(values[j], weights[j], preferred_element_type=jnp.float32)


def mix(pick, use, start, coeff, pieces):
    neigh = coeff.shape[1]
    rows, cols = start.shape
    vmem = pl.BlockSpec(memory_space=pltpu.VMEM)
    smem = pl.BlockSpec(memory_space=pltpu.SMEM)
    anywhere = pl.BlockSpec(memory_space=pl.ANY)
    return pl.pallas_call(
        functools.partial(mix_kernel, len(pieces), neigh),
        out_shape=jax.ShapeDtypeStruct((rows, cols), jnp.float32),
        in_specs=[smem, smem, vmem, anywhere] + [anywhere] * len(pieces),
        out_specs=vmem,
        scratch_shapes=[
            pltpu.VMEM((neigh, rows, coeff.shape[2]), pieces[0].dtype),
            pltpu.VMEM(coeff.shape[1:], coeff.dtype),
            pltpu.SemaphoreType.DMA((2, neigh)),
        ],
        cost_estimate=pl.CostEstimate(
            flops=2 * rows * cols * coeff.shape[2] * neigh,
            bytes_accessed=(2 * neigh + 2) * rows * cols * 4 + coeff.size * 2,
            transcendentals=0,
        ),
    )(pick, use, start, coeff, *pieces)


def body(coeff, solve, noise, prior, owner, nbrs):
    part_size = lax.axis_size("blk")
    space_index = lax.axis_index("space")
    blk_index = lax.axis_index("blk")
    own_slot = space_index * part_size + blk_index
    count = owner.shape[0]
    block_ids = jnp.arange(count, dtype=jnp.int32)
    levels = block_levels(nbrs, count)
    own_block = jnp.sum(jnp.where(owner == own_slot, block_ids, 0))
    own_level = jnp.sum(jnp.where(block_ids == own_block, levels, 0))
    own_list = jnp.sum(jnp.where((block_ids == own_block)[:, None], nbrs, 0), axis=0)
    is_current = (own_list >= count).astype(jnp.int32)
    target = jnp.remainder(own_list, count)
    near_slot = jnp.sum(jnp.where(target[:, None] == block_ids[None, :], owner[None, :], 0), axis=1)
    distance = near_slot // part_size - space_index
    offset = jnp.remainder(near_slot - blk_index, part_size)
    pick = ((distance + REACH) * part_size + offset).astype(jnp.int32)

    arrives = jnp.where(is_current != 0, jnp.sum(jnp.where(target[:, None] == block_ids[None, :], levels[None, :], 0), axis=1) + 1, 0)
    every_slot = owner[:, None]
    listed = jnp.remainder(nbrs, count)[:, :, None] == block_ids[None, None, :]
    listed_slot = jnp.sum(jnp.where(listed, owner[None, None, :], 0), axis=2)
    listed_distance = listed_slot // part_size - every_slot // part_size + REACH
    listed_level = jnp.sum(jnp.where(listed, levels[None, None, :], 0), axis=2)
    listed_round = jnp.where(nbrs >= count, listed_level + 1, 0)
    rounds = jnp.arange(LEVELS, dtype=jnp.int32)
    groups = jnp.arange(2 * REACH + 1, dtype=jnp.int32)
    remote = listed_slot != every_slot
    hits = (listed_round[:, :, None, None] == rounds[:, None]) & (listed_distance[:, :, None, None] == groups[None, :])
    need = jnp.max(jnp.where(hits & remote[:, :, None, None], 1, 0), axis=(0, 1)).astype(jnp.int32)
    if lax.axis_size("groups") == 2:
        need = jnp.maximum(need, lax.ppermute(need, "groups", [(0, 1), (1, 0)]))
    else:
        need = lax.pmax(need, "groups")
    pattern = jnp.sum(need * (2 ** groups)[None, :], axis=1)

    prior_pieces = neighbourhood(prior[0])
    acc = mix(pick, 1 - is_current, noise[0], coeff, prior_pieces)

    def unchanged(previous):
        return previous

    def finished(block, total):
        right_side = total.astype(jnp.bfloat16)
        return jnp.dot(right_side, solve[0], preferred_element_type=jnp.float32).astype(jnp.bfloat16)

    def exchange(chosen, level_now, carry):
        block, total = carry
        space_count = lax.axis_size("space")
        pieces = []
        for distance in range(-REACH, REACH + 1):
            for offset in range(part_size):
                if (distance == 0 and offset == 0) or not chosen & (1 << (distance + REACH)):
                    pieces.append(block)
                    continue
                pairs = window_pairs(space_count, part_size, distance, offset)
                pieces.append(lax.ppermute(block, ("space", "blk"), pairs))
        use = (arrives == level_now).astype(jnp.int32)
        total = mix(pick, use, total, coeff, pieces)
        block = lax.cond(own_level == level_now, functools.partial(finished, total=total), unchanged, block)
        return block, total

    current = lax.cond(own_level == 0, functools.partial(finished, total=acc), unchanged, jnp.zeros_like(prior[0]))
    every_group = 2 ** (2 * REACH + 1) - 1
    for level_now in range(1, LEVELS):
        if level_now == 2:
            branches = [unchanged] + [
                functools.partial(exchange, chosen, level_now) for chosen in range(1, every_group + 1)
            ]
            current, acc = lax.switch(pattern[level_now], branches, (current, acc))
        else:
            whole = functools.partial(exchange, every_group, level_now)
            current, acc = lax.cond(pattern[level_now] > 0, whole, unchanged, (current, acc))
    return current[None]


def solution(mesh):
    placed = (
        P(("groups", "space", "blk"), None, None, None),
        P(("groups", "space", "blk"), None, None),
        P(("groups", "space", "blk"), "samp", None),
        P(("groups", "space", "blk"), "samp", None),
        P("groups"),
        P("groups", None),
    )
    return jax.shard_map(
        body,
        mesh=mesh,
        in_specs=placed,
        out_specs=P(("groups", "space", "blk"), "samp", None),
        check_vma=False,
    )
```

```python
import functools

import jax
import jax.numpy as jnp
from jax import lax
from jax.experimental import pallas as pl
from jax.experimental.pallas import tpu as pltpu
from jax.sharding import PartitionSpec as P

LEVELS = 4
REACH = 1


def block_levels(nbrs, count):
    block_ids = jnp.arange(count, dtype=jnp.int32)
    is_current = nbrs >= count
    target = jnp.remainder(nbrs, count)
    picks = target[:, :, None] == block_ids[None, None, :]
    levels = jnp.zeros((count,), jnp.int32)
    for sweep in range(LEVELS):
        looked = jnp.sum(jnp.where(picks, levels[None, None, :], 0), axis=2)
        above = jnp.where(is_current, looked + 1, 0)
        levels = jnp.max(above, axis=1)
    return levels


def window_pairs(space_count, part_size, distance, offset):
    pairs = []
    for space_to in range(space_count):
        space_from = space_to + distance
        if not 0 <= space_from < space_count:
            continue
        for blk_to in range(part_size):
            blk_from = (blk_to + offset) % part_size
            pairs.append((space_from * part_size + blk_from, space_to * part_size + blk_to))
    return pairs


def neighbourhood(local_block):
    part_size = lax.axis_size("blk")
    space_count = lax.axis_size("space")
    pieces = []
    for distance in range(-REACH, REACH + 1):
        for offset in range(part_size):
            if distance == 0 and offset == 0:
                pieces.append(local_block)
                continue
            pairs = window_pairs(space_count, part_size, distance, offset)
            pieces.append(lax.ppermute(local_block, ("space", "blk"), pairs))
    return pieces


def mix_kernel(n_pieces, neigh, pick_ref, use_ref, start_ref, coeff_hbm, *rest):
    pieces = rest[:n_pieces]
    out_ref, values, weights, sems = rest[n_pieces:]
    for j in range(neigh):

        @pl.when(use_ref[j] != 0)
        def _():
            pltpu.make_async_copy(coeff_hbm.at[0, j], weights.at[j], sems.at[1, j]).start()

        for p in range(n_pieces):

            @pl.when((pick_ref[j] == p) & (use_ref[j] != 0))
            def _():
                pltpu.make_async_copy(pieces[p], values.at[j], sems.at[0, j]).start()

    out_ref[...] = start_ref[...]
    for j in range(neigh):

        @pl.when(use_ref[j] != 0)
        def _():
            pltpu.make_async_copy(pieces[0], values.at[j], sems.at[0, j]).wait()
            pltpu.make_async_copy(coeff_hbm.at[0, j], weights.at[j], sems.at[1, j]).wait()
            out_ref[...] -= jnp.dot(values[j], weights[j], preferred_element_type=jnp.float32)


def mix(pick, use, start, coeff, pieces):
    neigh = coeff.shape[1]
    rows, cols = start.shape
    vmem = pl.BlockSpec(memory_space=pltpu.VMEM)
    smem = pl.BlockSpec(memory_space=pltpu.SMEM)
    anywhere = pl.BlockSpec(memory_space=pl.ANY)
    return pl.pallas_call(
        functools.partial(mix_kernel, len(pieces), neigh),
        out_shape=jax.ShapeDtypeStruct((rows, cols), jnp.float32),
        in_specs=[smem, smem, vmem, anywhere] + [anywhere] * len(pieces),
        out_specs=vmem,
        scratch_shapes=[
            pltpu.VMEM((neigh, rows, coeff.shape[2]), pieces[0].dtype),
            pltpu.VMEM(coeff.shape[1:], coeff.dtype),
            pltpu.SemaphoreType.DMA((2, neigh)),
        ],
        cost_estimate=pl.CostEstimate(
            flops=2 * rows * cols * coeff.shape[2] * neigh,
            bytes_accessed=(2 * neigh + 2) * rows * cols * 4 + coeff.size * 2,
            transcendentals=0,
        ),
    )(pick, use, start, coeff, *pieces)


def step_kernel(n_pieces, neigh, pick_ref, use_ref, flag_ref, total_hbm, block_hbm, coeff_hbm, solve_hbm, *rest):
    pieces = rest[:n_pieces]
    total_ref, block_ref, values, weights, solve_v, sems, own_sems = rest[n_pieces:]
    take_total = pltpu.make_async_copy(total_hbm, total_ref, own_sems.at[0])
    take_total.start()
    for j in range(neigh):

        @pl.when(use_ref[j] != 0)
        def _():
            pltpu.make_async_copy(coeff_hbm.at[0, j], weights.at[j], sems.at[1, j]).start()

        for p in range(n_pieces):

            @pl.when((pick_ref[j] == p) & (use_ref[j] != 0))
            def _():
                pltpu.make_async_copy(pieces[p], values.at[j], sems.at[0, j]).start()

    take_solve = pltpu.make_async_copy(solve_hbm.at[0], solve_v, own_sems.at[1])
    take_block = pltpu.make_async_copy(block_hbm, block_ref, own_sems.at[2])

    @pl.when(flag_ref[0] != 0)
    def _():
        take_solve.start()

    @pl.when(flag_ref[0] == 0)
    def _():
        take_block.start()

    take_total.wait()
    for j in range(neigh):

        @pl.when(use_ref[j] != 0)
        def _():
            pltpu.make_async_copy(pieces[0], values.at[j], sems.at[0, j]).wait()
            pltpu.make_async_copy(coeff_hbm.at[0, j], weights.at[j], sems.at[1, j]).wait()
            total_ref[...] -= jnp.dot(values[j], weights[j], preferred_element_type=jnp.float32)

    @pl.when(flag_ref[0] != 0)
    def _():
        take_solve.wait()
        right_side = total_ref[...].astype(jnp.bfloat16)
        block_ref[...] = jnp.dot(right_side, solve_v[...], preferred_element_type=jnp.float32).astype(block_ref.dtype)

    @pl.when(flag_ref[0] == 0)
    def _():
        take_block.wait()


def step(pick, use, flag, total, block, coeff, solve, pieces):
    neigh = coeff.shape[1]
    rows, cols = total.shape
    vmem = pl.BlockSpec(memory_space=pltpu.VMEM)
    smem = pl.BlockSpec(memory_space=pltpu.SMEM)
    anywhere = pl.BlockSpec(memory_space=pl.ANY)
    return pl.pallas_call(
        functools.partial(step_kernel, len(pieces), neigh),
        out_shape=(jax.ShapeDtypeStruct((rows, cols), jnp.float32), jax.ShapeDtypeStruct((rows, cols), block.dtype)),
        in_specs=[smem, smem, smem] + [anywhere] * (4 + len(pieces)),
        out_specs=(vmem, vmem),
        scratch_shapes=[
            pltpu.VMEM((neigh, rows, coeff.shape[2]), pieces[0].dtype),
            pltpu.VMEM(coeff.shape[1:], coeff.dtype),
            pltpu.VMEM(solve.shape[1:], solve.dtype),
            pltpu.SemaphoreType.DMA((2, neigh)),
            pltpu.SemaphoreType.DMA((3,)),
        ],
        cost_estimate=pl.CostEstimate(
            flops=2 * rows * cols * coeff.shape[2] * (neigh + 1),
            bytes_accessed=(2 * neigh + 4) * rows * cols * 4 + coeff.size * 2,
            transcendentals=0,
        ),
    )(pick, use, flag, total, block, coeff, solve, *pieces)


def body(coeff, solve, noise, prior, owner, nbrs):
    part_size = lax.axis_size("blk")
    space_index = lax.axis_index("space")
    blk_index = lax.axis_index("blk")
    own_slot = space_index * part_size + blk_index
    count = owner.shape[0]
    block_ids = jnp.arange(count, dtype=jnp.int32)
    levels = block_levels(nbrs, count)
    own_block = jnp.sum(jnp.where(owner == own_slot, block_ids, 0))
    own_level = jnp.sum(jnp.where(block_ids == own_block, levels, 0))
    own_list = jnp.sum(jnp.where((block_ids == own_block)[:, None], nbrs, 0), axis=0)
    is_current = (own_list >= count).astype(jnp.int32)
    target = jnp.remainder(own_list, count)
    near_slot = jnp.sum(jnp.where(target[:, None] == block_ids[None, :], owner[None, :], 0), axis=1)
    distance = near_slot // part_size - space_index
    offset = jnp.remainder(near_slot - blk_index, part_size)
    pick = ((distance + REACH) * part_size + offset).astype(jnp.int32)

    arrives = jnp.where(is_current != 0, jnp.sum(jnp.where(target[:, None] == block_ids[None, :], levels[None, :], 0), axis=1) + 1, 0)
    every_slot = owner[:, None]
    listed = jnp.remainder(nbrs, count)[:, :, None] == block_ids[None, None, :]
    listed_slot = jnp.sum(jnp.where(listed, owner[None, None, :], 0), axis=2)
    listed_distance = listed_slot // part_size - every_slot // part_size + REACH
    listed_level = jnp.sum(jnp.where(listed, levels[None, None, :], 0), axis=2)
    listed_round = jnp.where(nbrs >= count, listed_level + 1, 0)
    rounds = jnp.arange(LEVELS, dtype=jnp.int32)
    groups = jnp.arange(2 * REACH + 1, dtype=jnp.int32)
    remote = listed_slot != every_slot
    hits = (listed_round[:, :, None, None] == rounds[:, None]) & (listed_distance[:, :, None, None] == groups[None, :])
    need = jnp.max(jnp.where(hits & remote[:, :, None, None], 1, 0), axis=(0, 1)).astype(jnp.int32)
    if lax.axis_size("groups") == 2:
        need = jnp.maximum(need, lax.ppermute(need, "groups", [(0, 1), (1, 0)]))
    else:
        need = lax.pmax(need, "groups")
    pattern = jnp.sum(need * (2 ** groups)[None, :], axis=1)

    prior_pieces = neighbourhood(prior[0])
    acc = mix(pick, 1 - is_current, noise[0], coeff, prior_pieces)

    def unchanged(previous):
        return previous

    def finished(block, total):
        right_side = total.astype(jnp.bfloat16)
        return jnp.dot(right_side, solve[0], preferred_element_type=jnp.float32).astype(jnp.bfloat16)

    def exchange(chosen, level_now, carry):
        block, total = carry
        space_count = lax.axis_size("space")
        pieces = []
        for distance in range(-REACH, REACH + 1):
            for offset in range(part_size):
                if (distance == 0 and offset == 0) or not chosen & (1 << (distance + REACH)):
                    pieces.append(block)
                    continue
                pairs = window_pairs(space_count, part_size, distance, offset)
                pieces.append(lax.ppermute(block, ("space", "blk"), pairs))
        use = (arrives == level_now).astype(jnp.int32)
        flag = (own_level == level_now).astype(jnp.int32)[None]
        total, block = step(pick, use, flag, total, block, coeff, solve, pieces)
        return block, total

    current = lax.cond(own_level == 0, functools.partial(finished, total=acc), unchanged, jnp.zeros_like(prior[0]))
    every_group = 2 ** (2 * REACH + 1) - 1
    for level_now in range(1, LEVELS):
        if level_now == 2:
            branches = [unchanged] + [
                functools.partial(exchange, chosen, level_now) for chosen in range(1, every_group + 1)
            ]
            current, acc = lax.switch(pattern[level_now], branches, (current, acc))
        else:
            whole = functools.partial(exchange, every_group, level_now)
            current, acc = lax.cond(pattern[level_now] > 0, whole, unchanged, (current, acc))
    return current[None]


def solution(mesh):
    placed = (
        P(("groups", "space", "blk"), None, None, None),
        P(("groups", "space", "blk"), None, None),
        P(("groups", "space", "blk"), "samp", None),
        P(("groups", "space", "blk"), "samp", None),
        P("groups"),
        P("groups", None),
    )
    return jax.shard_map(
        body,
        mesh=mesh,
        in_specs=placed,
        out_specs=P(("groups", "space", "blk"), "samp", None),
        check_vma=False,
    )
```

```python
import functools

import jax
import jax.numpy as jnp
from jax import lax
from jax.experimental import pallas as pl
from jax.experimental.pallas import tpu as pltpu
from jax.sharding import PartitionSpec as P

LEVELS = 4
REACH = 1


def block_levels(nbrs, count):
    block_ids = jnp.arange(count, dtype=jnp.int32)
    is_current = nbrs >= count
    target = jnp.remainder(nbrs, count)
    picks = target[:, :, None] == block_ids[None, None, :]
    levels = jnp.zeros((count,), jnp.int32)
    for sweep in range(LEVELS):
        looked = jnp.sum(jnp.where(picks, levels[None, None, :], 0), axis=2)
        above = jnp.where(is_current, looked + 1, 0)
        levels = jnp.max(above, axis=1)
    return levels


def window_pairs(space_count, part_size, distance, offset):
    pairs = []
    for space_to in range(space_count):
        space_from = space_to + distance
        if not 0 <= space_from < space_count:
            continue
        for blk_to in range(part_size):
            blk_from = (blk_to + offset) % part_size
            pairs.append((space_from * part_size + blk_from, space_to * part_size + blk_to))
    return pairs


def neighbourhood(local_block):
    part_size = lax.axis_size("blk")
    space_count = lax.axis_size("space")
    pieces = []
    for distance in range(-REACH, REACH + 1):
        for offset in range(part_size):
            if distance == 0 and offset == 0:
                pieces.append(local_block)
                continue
            pairs = window_pairs(space_count, part_size, distance, offset)
            pieces.append(lax.ppermute(local_block, ("space", "blk"), pairs))
    return pieces


def mix_kernel(n_pieces, neigh, pick_ref, use_ref, start_ref, coeff_hbm, *rest):
    pieces = rest[:n_pieces]
    out_ref, values, weights, sems = rest[n_pieces:]
    for j in range(neigh):

        @pl.when(use_ref[j] != 0)
        def _():
            pltpu.make_async_copy(coeff_hbm.at[0, j], weights.at[j], sems.at[1, j]).start()

        for p in range(n_pieces):

            @pl.when((pick_ref[j] == p) & (use_ref[j] != 0))
            def _():
                pltpu.make_async_copy(pieces[p], values.at[j], sems.at[0, j]).start()

    out_ref[...] = start_ref[...]
    for j in range(neigh):

        @pl.when(use_ref[j] != 0)
        def _():
            pltpu.make_async_copy(pieces[0], values.at[j], sems.at[0, j]).wait()
            pltpu.make_async_copy(coeff_hbm.at[0, j], weights.at[j], sems.at[1, j]).wait()
            out_ref[...] -= jnp.dot(values[j], weights[j], preferred_element_type=jnp.float32)


def mix(pick, use, start, coeff, pieces):
    neigh = coeff.shape[1]
    rows, cols = start.shape
    vmem = pl.BlockSpec(memory_space=pltpu.VMEM)
    smem = pl.BlockSpec(memory_space=pltpu.SMEM)
    anywhere = pl.BlockSpec(memory_space=pl.ANY)
    return pl.pallas_call(
        functools.partial(mix_kernel, len(pieces), neigh),
        out_shape=jax.ShapeDtypeStruct((rows, cols), jnp.float32),
        in_specs=[smem, smem, vmem, anywhere] + [anywhere] * len(pieces),
        out_specs=vmem,
        scratch_shapes=[
            pltpu.VMEM((neigh, rows, coeff.shape[2]), pieces[0].dtype),
            pltpu.VMEM(coeff.shape[1:], coeff.dtype),
            pltpu.SemaphoreType.DMA((2, neigh)),
        ],
        cost_estimate=pl.CostEstimate(
            flops=2 * rows * cols * coeff.shape[2] * neigh,
            bytes_accessed=(2 * neigh + 2) * rows * cols * 4 + coeff.size * 2,
            transcendentals=0,
        ),
    )(pick, use, start, coeff, *pieces)


def step_kernel(n_pieces, neigh, pick_ref, use_ref, flag_ref, total_hbm, block_hbm, coeff_hbm, solve_hbm, *rest):
    pieces = rest[:n_pieces]
    total_ref, block_ref, values, weights, solve_v, sems, own_sems = rest[n_pieces:]
    take_total = pltpu.make_async_copy(total_hbm, total_ref, own_sems.at[0])
    take_total.start()
    for j in range(neigh):

        @pl.when(use_ref[j] != 0)
        def _():
            pltpu.make_async_copy(coeff_hbm.at[0, j], weights.at[j], sems.at[1, j]).start()

        for p in range(n_pieces):

            @pl.when((pick_ref[j] == p) & (use_ref[j] != 0))
            def _():
                pltpu.make_async_copy(pieces[p], values.at[j], sems.at[0, j]).start()

    take_solve = pltpu.make_async_copy(solve_hbm.at[0], solve_v, own_sems.at[1])
    take_block = pltpu.make_async_copy(block_hbm, block_ref, own_sems.at[2])

    @pl.when(flag_ref[0] != 0)
    def _():
        take_solve.start()

    @pl.when(flag_ref[0] == 0)
    def _():
        take_block.start()

    take_total.wait()
    for j in range(neigh):

        @pl.when(use_ref[j] != 0)
        def _():
            pltpu.make_async_copy(pieces[0], values.at[j], sems.at[0, j]).wait()
            pltpu.make_async_copy(coeff_hbm.at[0, j], weights.at[j], sems.at[1, j]).wait()
            total_ref[...] -= jnp.dot(values[j], weights[j], preferred_element_type=jnp.float32)

    @pl.when(flag_ref[0] != 0)
    def _():
        take_solve.wait()
        right_side = total_ref[...].astype(jnp.bfloat16)
        block_ref[...] = jnp.dot(right_side, solve_v[...], preferred_element_type=jnp.float32).astype(block_ref.dtype)

    @pl.when(flag_ref[0] == 0)
    def _():
        take_block.wait()


def step(pick, use, flag, total, block, coeff, solve, pieces):
    neigh = coeff.shape[1]
    rows, cols = total.shape
    vmem = pl.BlockSpec(memory_space=pltpu.VMEM)
    smem = pl.BlockSpec(memory_space=pltpu.SMEM)
    anywhere = pl.BlockSpec(memory_space=pl.ANY)
    return pl.pallas_call(
        functools.partial(step_kernel, len(pieces), neigh),
        out_shape=(jax.ShapeDtypeStruct((rows, cols), jnp.float32), jax.ShapeDtypeStruct((rows, cols), block.dtype)),
        in_specs=[smem, smem, smem] + [anywhere] * (4 + len(pieces)),
        out_specs=(vmem, vmem),
        scratch_shapes=[
            pltpu.VMEM((neigh, rows, coeff.shape[2]), pieces[0].dtype),
            pltpu.VMEM(coeff.shape[1:], coeff.dtype),
            pltpu.VMEM(solve.shape[1:], solve.dtype),
            pltpu.SemaphoreType.DMA((2, neigh)),
            pltpu.SemaphoreType.DMA((3,)),
        ],
        cost_estimate=pl.CostEstimate(
            flops=2 * rows * cols * coeff.shape[2] * (neigh + 1),
            bytes_accessed=(2 * neigh + 4) * rows * cols * 4 + coeff.size * 2,
            transcendentals=0,
        ),
    )(pick, use, flag, total, block, coeff, solve, *pieces)


def body(coeff, solve, noise, prior, owner, nbrs):
    part_size = lax.axis_size("blk")
    space_index = lax.axis_index("space")
    blk_index = lax.axis_index("blk")
    own_slot = space_index * part_size + blk_index
    count = owner.shape[0]
    block_ids = jnp.arange(count, dtype=jnp.int32)
    levels = block_levels(nbrs, count)
    own_block = jnp.sum(jnp.where(owner == own_slot, block_ids, 0))
    own_level = jnp.sum(jnp.where(block_ids == own_block, levels, 0))
    own_list = jnp.sum(jnp.where((block_ids == own_block)[:, None], nbrs, 0), axis=0)
    is_current = (own_list >= count).astype(jnp.int32)
    target = jnp.remainder(own_list, count)
    near_slot = jnp.sum(jnp.where(target[:, None] == block_ids[None, :], owner[None, :], 0), axis=1)
    distance = near_slot // part_size - space_index
    offset = jnp.remainder(near_slot - blk_index, part_size)
    pick = ((distance + REACH) * part_size + offset).astype(jnp.int32)

    arrives = jnp.where(is_current != 0, jnp.sum(jnp.where(target[:, None] == block_ids[None, :], levels[None, :], 0), axis=1) + 1, 0)
    every_slot = owner[:, None]
    listed = jnp.remainder(nbrs, count)[:, :, None] == block_ids[None, None, :]
    listed_slot = jnp.sum(jnp.where(listed, owner[None, None, :], 0), axis=2)
    listed_distance = listed_slot // part_size - every_slot // part_size + REACH
    listed_level = jnp.sum(jnp.where(listed, levels[None, None, :], 0), axis=2)
    listed_round = jnp.where(nbrs >= count, listed_level + 1, 0)
    rounds = jnp.arange(LEVELS, dtype=jnp.int32)
    groups = jnp.arange(2 * REACH + 1, dtype=jnp.int32)
    remote = listed_slot != every_slot
    hits = (listed_round[:, :, None, None] == rounds[:, None]) & (listed_distance[:, :, None, None] == groups[None, :])
    need = jnp.max(jnp.where(hits & remote[:, :, None, None], 1, 0), axis=(0, 1)).astype(jnp.int32)
    if lax.axis_size("groups") == 2:
        need = jnp.maximum(need, lax.ppermute(need, "groups", [(0, 1), (1, 0)]))
    else:
        need = lax.pmax(need, "groups")
    pattern = jnp.sum(need * (2 ** groups)[None, :], axis=1)

    prior_pieces = neighbourhood(prior[0])

    def unchanged(previous):
        return previous

    def finished(block, total):
        right_side = total.astype(jnp.bfloat16)
        return jnp.dot(right_side, solve[0], preferred_element_type=jnp.float32).astype(jnp.bfloat16)

    def exchange(chosen, level_now, carry):
        block, total = carry
        space_count = lax.axis_size("space")
        pieces = []
        for distance in range(-REACH, REACH + 1):
            for offset in range(part_size):
                if (distance == 0 and offset == 0) or not chosen & (1 << (distance + REACH)):
                    pieces.append(prior_pieces[len(pieces)])
                    continue
                pairs = window_pairs(space_count, part_size, distance, offset)
                pieces.append(lax.ppermute(block, ("space", "blk"), pairs))
        use = (arrives == level_now).astype(jnp.int32)
        flag = (own_level == level_now).astype(jnp.int32)[None]
        total, block = step(pick, use, flag, total, block, coeff, solve, pieces)
        return block, total

    first = (own_level == 0).astype(jnp.int32)[None]
    acc, current = step(pick, 1 - is_current, first, noise[0], prior[0], coeff, solve, prior_pieces)
    every_group = 2 ** (2 * REACH + 1) - 1
    for level_now in range(1, LEVELS):
        if level_now == 2:
            branches = [unchanged] + [
                functools.partial(exchange, chosen, level_now) for chosen in range(1, every_group + 1)
            ]
            current, acc = lax.switch(pattern[level_now], branches, (current, acc))
        else:
            whole = functools.partial(exchange, every_group, level_now)
            current, acc = lax.cond(pattern[level_now] > 0, whole, unchanged, (current, acc))
    return current[None]


def solution(mesh):
    placed = (
        P(("groups", "space", "blk"), None, None, None),
        P(("groups", "space", "blk"), None, None),
        P(("groups", "space", "blk"), "samp", None),
        P(("groups", "space", "blk"), "samp", None),
        P("groups"),
        P("groups", None),
    )
    return jax.shard_map(
        body,
        mesh=mesh,
        in_specs=placed,
        out_specs=P(("groups", "space", "blk"), "samp", None),
        check_vma=False,
    )
```

```python
import functools

import jax
import jax.numpy as jnp
from jax import lax
from jax.experimental import pallas as pl
from jax.experimental.pallas import tpu as pltpu
from jax.sharding import PartitionSpec as P

LEVELS = 4
REACH = 1


def block_levels(nbrs, count):
    block_ids = jnp.arange(count, dtype=jnp.int32)
    is_current = nbrs >= count
    target = jnp.remainder(nbrs, count)
    picks = target[:, :, None] == block_ids[None, None, :]
    levels = jnp.zeros((count,), jnp.int32)
    for sweep in range(LEVELS):
        looked = jnp.sum(jnp.where(picks, levels[None, None, :], 0), axis=2)
        above = jnp.where(is_current, looked + 1, 0)
        levels = jnp.max(above, axis=1)
    return levels


def window_pairs(space_count, part_size, distance, offset):
    pairs = []
    for space_to in range(space_count):
        space_from = space_to + distance
        if not 0 <= space_from < space_count:
            continue
        for blk_to in range(part_size):
            blk_from = (blk_to + offset) % part_size
            pairs.append((space_from * part_size + blk_from, space_to * part_size + blk_to))
    return pairs


def neighbourhood(local_block):
    part_size = lax.axis_size("blk")
    space_count = lax.axis_size("space")
    pieces = []
    for distance in range(-REACH, REACH + 1):
        for offset in range(part_size):
            if distance == 0 and offset == 0:
                pieces.append(local_block)
                continue
            pairs = window_pairs(space_count, part_size, distance, offset)
            pieces.append(lax.ppermute(local_block, ("space", "blk"), pairs))
    return pieces


def mix_kernel(n_pieces, neigh, pick_ref, use_ref, start_ref, coeff_hbm, *rest):
    pieces = rest[:n_pieces]
    out_ref, values, weights, sems = rest[n_pieces:]
    for j in range(neigh):

        @pl.when(use_ref[j] != 0)
        def _():
            pltpu.make_async_copy(coeff_hbm.at[0, j], weights.at[j], sems.at[1, j]).start()

        for p in range(n_pieces):

            @pl.when((pick_ref[j] == p) & (use_ref[j] != 0))
            def _():
                pltpu.make_async_copy(pieces[p], values.at[j], sems.at[0, j]).start()

    out_ref[...] = start_ref[...]
    for j in range(neigh):

        @pl.when(use_ref[j] != 0)
        def _():
            pltpu.make_async_copy(pieces[0], values.at[j], sems.at[0, j]).wait()
            pltpu.make_async_copy(coeff_hbm.at[0, j], weights.at[j], sems.at[1, j]).wait()
            out_ref[...] -= jnp.dot(values[j], weights[j], preferred_element_type=jnp.float32)


def mix(pick, use, start, coeff, pieces):
    neigh = coeff.shape[1]
    rows, cols = start.shape
    vmem = pl.BlockSpec(memory_space=pltpu.VMEM)
    smem = pl.BlockSpec(memory_space=pltpu.SMEM)
    anywhere = pl.BlockSpec(memory_space=pl.ANY)
    return pl.pallas_call(
        functools.partial(mix_kernel, len(pieces), neigh),
        out_shape=jax.ShapeDtypeStruct((rows, cols), jnp.float32),
        in_specs=[smem, smem, vmem, anywhere] + [anywhere] * len(pieces),
        out_specs=vmem,
        scratch_shapes=[
            pltpu.VMEM((neigh, rows, coeff.shape[2]), pieces[0].dtype),
            pltpu.VMEM(coeff.shape[1:], coeff.dtype),
            pltpu.SemaphoreType.DMA((2, neigh)),
        ],
        cost_estimate=pl.CostEstimate(
            flops=2 * rows * cols * coeff.shape[2] * neigh,
            bytes_accessed=(2 * neigh + 2) * rows * cols * 4 + coeff.size * 2,
            transcendentals=0,
        ),
    )(pick, use, start, coeff, *pieces)


def step_kernel(n_pieces, neigh, pick_ref, use_ref, flag_ref, total_hbm, block_hbm, coeff_hbm, solve_hbm, *rest):
    pieces = rest[:n_pieces]
    total_out, block_out, total_v, block_v, values, weights, solve_v, sems, own_sems = rest[n_pieces:]
    take_total = pltpu.make_async_copy(total_hbm, total_v, own_sems.at[0])
    take_total.start()
    for j in range(neigh):

        @pl.when(use_ref[j] != 0)
        def _():
            pltpu.make_async_copy(coeff_hbm.at[0, j], weights.at[j], sems.at[1, j]).start()

        for p in range(n_pieces):

            @pl.when((pick_ref[j] == p) & (use_ref[j] != 0))
            def _():
                pltpu.make_async_copy(pieces[p], values.at[j], sems.at[0, j]).start()

    take_solve = pltpu.make_async_copy(solve_hbm.at[0], solve_v, own_sems.at[1])

    @pl.when(flag_ref[0] != 0)
    def _():
        take_solve.start()

    take_total.wait()
    for j in range(neigh):

        @pl.when(use_ref[j] != 0)
        def _():
            pltpu.make_async_copy(pieces[0], values.at[j], sems.at[0, j]).wait()
            pltpu.make_async_copy(coeff_hbm.at[0, j], weights.at[j], sems.at[1, j]).wait()
            total_v[...] -= jnp.dot(values[j], weights[j], preferred_element_type=jnp.float32)

    put_total = pltpu.make_async_copy(total_v, total_out, own_sems.at[3])
    put_total.start()

    @pl.when(flag_ref[0] != 0)
    def _():
        take_solve.wait()
        right_side = total_v[...].astype(jnp.bfloat16)
        block_v[...] = jnp.dot(right_side, solve_v[...], preferred_element_type=jnp.float32).astype(block_v.dtype)

        put_block = pltpu.make_async_copy(block_v, block_out, own_sems.at[4])
        put_block.start()
        put_block.wait()

    put_total.wait()


def step(pick, use, flag, total, block, coeff, solve, pieces):
    neigh = coeff.shape[1]
    rows, cols = total.shape
    smem = pl.BlockSpec(memory_space=pltpu.SMEM)
    anywhere = pl.BlockSpec(memory_space=pl.ANY)
    return pl.pallas_call(
        functools.partial(step_kernel, len(pieces), neigh),
        out_shape=(jax.ShapeDtypeStruct((rows, cols), jnp.float32), jax.ShapeDtypeStruct((rows, cols), block.dtype)),
        in_specs=[smem, smem, smem] + [anywhere] * (4 + len(pieces)),
        out_specs=(anywhere, anywhere),
        input_output_aliases={3: 0, 4: 1},
        scratch_shapes=[
            pltpu.VMEM((rows, cols), jnp.float32),
            pltpu.VMEM((rows, cols), block.dtype),
            pltpu.VMEM((neigh, rows, coeff.shape[2]), pieces[0].dtype),
            pltpu.VMEM(coeff.shape[1:], coeff.dtype),
            pltpu.VMEM(solve.shape[1:], solve.dtype),
            pltpu.SemaphoreType.DMA((2, neigh)),
            pltpu.SemaphoreType.DMA((5,)),
        ],
        cost_estimate=pl.CostEstimate(
            flops=2 * rows * cols * coeff.shape[2] * (neigh + 1),
            bytes_accessed=(2 * neigh + 4) * rows * cols * 4 + coeff.size * 2,
            transcendentals=0,
        ),
    )(pick, use, flag, total, block, coeff, solve, *pieces)


def body(coeff, solve, noise, prior, owner, nbrs):
    part_size = lax.axis_size("blk")
    space_index = lax.axis_index("space")
    blk_index = lax.axis_index("blk")
    own_slot = space_index * part_size + blk_index
    count = owner.shape[0]
    block_ids = jnp.arange(count, dtype=jnp.int32)
    levels = block_levels(nbrs, count)
    own_block = jnp.sum(jnp.where(owner == own_slot, block_ids, 0))
    own_level = jnp.sum(jnp.where(block_ids == own_block, levels, 0))
    own_list = jnp.sum(jnp.where((block_ids == own_block)[:, None], nbrs, 0), axis=0)
    is_current = (own_list >= count).astype(jnp.int32)
    target = jnp.remainder(own_list, count)
    near_slot = jnp.sum(jnp.where(target[:, None] == block_ids[None, :], owner[None, :], 0), axis=1)
    distance = near_slot // part_size - space_index
    offset = jnp.remainder(near_slot - blk_index, part_size)
    pick = ((distance + REACH) * part_size + offset).astype(jnp.int32)

    arrives = jnp.where(is_current != 0, jnp.sum(jnp.where(target[:, None] == block_ids[None, :], levels[None, :], 0), axis=1) + 1, 0)
    every_slot = owner[:, None]
    listed = jnp.remainder(nbrs, count)[:, :, None] == block_ids[None, None, :]
    listed_slot = jnp.sum(jnp.where(listed, owner[None, None, :], 0), axis=2)
    listed_distance = listed_slot // part_size - every_slot // part_size + REACH
    listed_level = jnp.sum(jnp.where(listed, levels[None, None, :], 0), axis=2)
    listed_round = jnp.where(nbrs >= count, listed_level + 1, 0)
    rounds = jnp.arange(LEVELS, dtype=jnp.int32)
    groups = jnp.arange(2 * REACH + 1, dtype=jnp.int32)
    remote = listed_slot != every_slot
    hits = (listed_round[:, :, None, None] == rounds[:, None]) & (listed_distance[:, :, None, None] == groups[None, :])
    need = jnp.max(jnp.where(hits & remote[:, :, None, None], 1, 0), axis=(0, 1)).astype(jnp.int32)
    if lax.axis_size("groups") == 2:
        need = jnp.maximum(need, lax.ppermute(need, "groups", [(0, 1), (1, 0)]))
    else:
        need = lax.pmax(need, "groups")
    pattern = jnp.sum(need * (2 ** groups)[None, :], axis=1)

    prior_pieces = neighbourhood(prior[0])

    def unchanged(previous):
        return previous

    def finished(block, total):
        right_side = total.astype(jnp.bfloat16)
        return jnp.dot(right_side, solve[0], preferred_element_type=jnp.float32).astype(jnp.bfloat16)

    def exchange(chosen, level_now, carry):
        block, total = carry
        space_count = lax.axis_size("space")
        pieces = []
        for distance in range(-REACH, REACH + 1):
            for offset in range(part_size):
                if (distance == 0 and offset == 0) or not chosen & (1 << (distance + REACH)):
                    pieces.append(prior_pieces[len(pieces)])
                    continue
                pairs = window_pairs(space_count, part_size, distance, offset)
                pieces.append(lax.ppermute(block, ("space", "blk"), pairs))
        use = (arrives == level_now).astype(jnp.int32)
        flag = (own_level == level_now).astype(jnp.int32)[None]
        total, block = step(pick, use, flag, total, block, coeff, solve, pieces)
        return block, total

    first = (own_level == 0).astype(jnp.int32)[None]
    acc, current = step(pick, 1 - is_current, first, noise[0], prior[0], coeff, solve, prior_pieces)
    every_group = 2 ** (2 * REACH + 1) - 1
    for level_now in range(1, LEVELS):
        if level_now == 2:
            branches = [unchanged] + [
                functools.partial(exchange, chosen, level_now) for chosen in range(1, every_group + 1)
            ]
            current, acc = lax.switch(pattern[level_now], branches, (current, acc))
        else:
            whole = functools.partial(exchange, every_group, level_now)
            current, acc = lax.cond(pattern[level_now] > 0, whole, unchanged, (current, acc))
    return current[None]


def solution(mesh):
    placed = (
        P(("groups", "space", "blk"), None, None, None),
        P(("groups", "space", "blk"), None, None),
        P(("groups", "space", "blk"), "samp", None),
        P(("groups", "space", "blk"), "samp", None),
        P("groups"),
        P("groups", None),
    )
    return jax.shard_map(
        body,
        mesh=mesh,
        in_specs=placed,
        out_specs=P(("groups", "space", "blk"), "samp", None),
        check_vma=False,
    )
```

```python
import functools

import jax
import jax.numpy as jnp
from jax import lax
from jax.experimental import pallas as pl
from jax.experimental.pallas import tpu as pltpu
from jax.sharding import PartitionSpec as P

LEVELS = 4
REACH = 1


def block_levels(nbrs, count):
    block_ids = jnp.arange(count, dtype=jnp.int32)
    is_current = nbrs >= count
    target = jnp.remainder(nbrs, count)
    picks = target[:, :, None] == block_ids[None, None, :]
    levels = jnp.zeros((count,), jnp.int32)
    for sweep in range(LEVELS):
        looked = jnp.sum(jnp.where(picks, levels[None, None, :], 0), axis=2)
        above = jnp.where(is_current, looked + 1, 0)
        levels = jnp.max(above, axis=1)
    return levels


def window_pairs(space_count, part_size, distance, offset):
    pairs = []
    for space_to in range(space_count):
        space_from = space_to + distance
        if not 0 <= space_from < space_count:
            continue
        for blk_to in range(part_size):
            blk_from = (blk_to + offset) % part_size
            pairs.append((space_from * part_size + blk_from, space_to * part_size + blk_to))
    return pairs


def neighbourhood(local_block):
    part_size = lax.axis_size("blk")
    space_count = lax.axis_size("space")
    pieces = []
    for distance in range(-REACH, REACH + 1):
        for offset in range(part_size):
            if distance == 0 and offset == 0:
                pieces.append(local_block)
                continue
            pairs = window_pairs(space_count, part_size, distance, offset)
            pieces.append(lax.ppermute(local_block, ("space", "blk"), pairs))
    return pieces


def mix_kernel(n_pieces, neigh, pick_ref, use_ref, start_ref, coeff_hbm, *rest):
    pieces = rest[:n_pieces]
    out_ref, values, weights, sems = rest[n_pieces:]
    for j in range(neigh):

        @pl.when(use_ref[j] != 0)
        def _():
            pltpu.make_async_copy(coeff_hbm.at[0, j], weights.at[j], sems.at[1, j]).start()

        for p in range(n_pieces):

            @pl.when((pick_ref[j] == p) & (use_ref[j] != 0))
            def _():
                pltpu.make_async_copy(pieces[p], values.at[j], sems.at[0, j]).start()

    out_ref[...] = start_ref[...]
    for j in range(neigh):

        @pl.when(use_ref[j] != 0)
        def _():
            pltpu.make_async_copy(pieces[0], values.at[j], sems.at[0, j]).wait()
            pltpu.make_async_copy(coeff_hbm.at[0, j], weights.at[j], sems.at[1, j]).wait()
            out_ref[...] -= jnp.dot(values[j], weights[j], preferred_element_type=jnp.float32)


def mix(pick, use, start, coeff, pieces):
    neigh = coeff.shape[1]
    rows, cols = start.shape
    vmem = pl.BlockSpec(memory_space=pltpu.VMEM)
    smem = pl.BlockSpec(memory_space=pltpu.SMEM)
    anywhere = pl.BlockSpec(memory_space=pl.ANY)
    return pl.pallas_call(
        functools.partial(mix_kernel, len(pieces), neigh),
        out_shape=jax.ShapeDtypeStruct((rows, cols), jnp.float32),
        in_specs=[smem, smem, vmem, anywhere] + [anywhere] * len(pieces),
        out_specs=vmem,
        scratch_shapes=[
            pltpu.VMEM((neigh, rows, coeff.shape[2]), pieces[0].dtype),
            pltpu.VMEM(coeff.shape[1:], coeff.dtype),
            pltpu.SemaphoreType.DMA((2, neigh)),
        ],
        cost_estimate=pl.CostEstimate(
            flops=2 * rows * cols * coeff.shape[2] * neigh,
            bytes_accessed=(2 * neigh + 2) * rows * cols * 4 + coeff.size * 2,
            transcendentals=0,
        ),
    )(pick, use, start, coeff, *pieces)


def step_kernel(n_pieces, neigh, pick_ref, use_ref, flag_ref, total_hbm, block_hbm, coeff_hbm, solve_hbm, *rest):
    pieces = rest[:n_pieces]
    total_out, block_out, total_v, block_v, values, weights, solve_v, sems, own_sems = rest[n_pieces:]
    take_total = pltpu.make_async_copy(total_hbm, total_v, own_sems.at[0])
    take_total.start()
    for j in range(neigh):

        @pl.when(use_ref[j] != 0)
        def _():
            pltpu.make_async_copy(coeff_hbm.at[0, j], weights.at[j], sems.at[1, j]).start()

        for p in range(n_pieces):

            @pl.when((pick_ref[j] == p) & (use_ref[j] != 0))
            def _():
                pltpu.make_async_copy(pieces[p], values.at[j], sems.at[0, j]).start()

    take_solve = pltpu.make_async_copy(solve_hbm.at[0], solve_v, own_sems.at[1])

    @pl.when(flag_ref[0] != 0)
    def _():
        take_solve.start()

    take_total.wait()
    for j in range(neigh):

        @pl.when(use_ref[j] != 0)
        def _():
            pltpu.make_async_copy(pieces[0], values.at[j], sems.at[0, j]).wait()
            pltpu.make_async_copy(coeff_hbm.at[0, j], weights.at[j], sems.at[1, j]).wait()
            total_v[...] -= jnp.dot(values[j], weights[j], preferred_element_type=jnp.float32)

    put_total = pltpu.make_async_copy(total_v, total_out, own_sems.at[3])
    put_total.start()

    @pl.when(flag_ref[0] != 0)
    def _():
        take_solve.wait()
        right_side = total_v[...].astype(jnp.bfloat16)
        block_v[...] = jnp.dot(right_side, solve_v[...], preferred_element_type=jnp.float32).astype(block_v.dtype)

        put_block = pltpu.make_async_copy(block_v, block_out, own_sems.at[4])
        put_block.start()
        put_block.wait()

    put_total.wait()


def step(pick, use, flag, total, block, coeff, solve, pieces, in_place=True):
    neigh = coeff.shape[1]
    rows, cols = total.shape
    smem = pl.BlockSpec(memory_space=pltpu.SMEM)
    anywhere = pl.BlockSpec(memory_space=pl.ANY)
    return pl.pallas_call(
        functools.partial(step_kernel, len(pieces), neigh),
        out_shape=(jax.ShapeDtypeStruct((rows, cols), jnp.float32), jax.ShapeDtypeStruct((rows, cols), block.dtype)),
        in_specs=[smem, smem, smem] + [anywhere] * (4 + len(pieces)),
        out_specs=(anywhere, anywhere),
        input_output_aliases={3: 0, 4: 1} if in_place else {},
        scratch_shapes=[
            pltpu.VMEM((rows, cols), jnp.float32),
            pltpu.VMEM((rows, cols), block.dtype),
            pltpu.VMEM((neigh, rows, coeff.shape[2]), pieces[0].dtype),
            pltpu.VMEM(coeff.shape[1:], coeff.dtype),
            pltpu.VMEM(solve.shape[1:], solve.dtype),
            pltpu.SemaphoreType.DMA((2, neigh)),
            pltpu.SemaphoreType.DMA((5,)),
        ],
        cost_estimate=pl.CostEstimate(
            flops=2 * rows * cols * coeff.shape[2] * (neigh + 1),
            bytes_accessed=(2 * neigh + 4) * rows * cols * 4 + coeff.size * 2,
            transcendentals=0,
        ),
    )(pick, use, flag, total, block, coeff, solve, *pieces)


def body(coeff, solve, noise, prior, owner, nbrs):
    part_size = lax.axis_size("blk")
    space_index = lax.axis_index("space")
    blk_index = lax.axis_index("blk")
    own_slot = space_index * part_size + blk_index
    count = owner.shape[0]
    block_ids = jnp.arange(count, dtype=jnp.int32)
    levels = block_levels(nbrs, count)
    own_block = jnp.sum(jnp.where(owner == own_slot, block_ids, 0))
    own_level = jnp.sum(jnp.where(block_ids == own_block, levels, 0))
    own_list = jnp.sum(jnp.where((block_ids == own_block)[:, None], nbrs, 0), axis=0)
    is_current = (own_list >= count).astype(jnp.int32)
    target = jnp.remainder(own_list, count)
    near_slot = jnp.sum(jnp.where(target[:, None] == block_ids[None, :], owner[None, :], 0), axis=1)
    distance = near_slot // part_size - space_index
    offset = jnp.remainder(near_slot - blk_index, part_size)
    pick = ((distance + REACH) * part_size + offset).astype(jnp.int32)

    arrives = jnp.where(is_current != 0, jnp.sum(jnp.where(target[:, None] == block_ids[None, :], levels[None, :], 0), axis=1) + 1, 0)
    every_slot = owner[:, None]
    listed = jnp.remainder(nbrs, count)[:, :, None] == block_ids[None, None, :]
    listed_slot = jnp.sum(jnp.where(listed, owner[None, None, :], 0), axis=2)
    listed_distance = listed_slot // part_size - every_slot // part_size + REACH
    listed_level = jnp.sum(jnp.where(listed, levels[None, None, :], 0), axis=2)
    listed_round = jnp.where(nbrs >= count, listed_level + 1, 0)
    rounds = jnp.arange(LEVELS, dtype=jnp.int32)
    groups = jnp.arange(2 * REACH + 1, dtype=jnp.int32)
    remote = listed_slot != every_slot
    hits = (listed_round[:, :, None, None] == rounds[:, None]) & (listed_distance[:, :, None, None] == groups[None, :])
    need = jnp.max(jnp.where(hits & remote[:, :, None, None], 1, 0), axis=(0, 1)).astype(jnp.int32)
    if lax.axis_size("groups") == 2:
        need = jnp.maximum(need, lax.ppermute(need, "groups", [(0, 1), (1, 0)]))
    else:
        need = lax.pmax(need, "groups")
    pattern = jnp.sum(need * (2 ** groups)[None, :], axis=1)

    prior_pieces = neighbourhood(prior[0])

    def unchanged(previous):
        return previous

    def finished(block, total):
        right_side = total.astype(jnp.bfloat16)
        return jnp.dot(right_side, solve[0], preferred_element_type=jnp.float32).astype(jnp.bfloat16)

    def exchange(chosen, level_now, carry):
        block, total = carry
        space_count = lax.axis_size("space")
        pieces = []
        for distance in range(-REACH, REACH + 1):
            for offset in range(part_size):
                if (distance == 0 and offset == 0) or not chosen & (1 << (distance + REACH)):
                    pieces.append(prior_pieces[len(pieces)])
                    continue
                pairs = window_pairs(space_count, part_size, distance, offset)
                pieces.append(lax.ppermute(block, ("space", "blk"), pairs))
        use = (arrives == level_now).astype(jnp.int32)
        flag = (own_level == level_now).astype(jnp.int32)[None]
        total, block = step(pick, use, flag, total, block, coeff, solve, pieces)
        return block, total

    first = (own_level == 0).astype(jnp.int32)[None]
    acc, current = step(pick, 1 - is_current, first, noise[0], prior[0], coeff, solve, prior_pieces, in_place=False)
    every_group = 2 ** (2 * REACH + 1) - 1
    for level_now in range(1, LEVELS):
        if level_now == 2:
            branches = [unchanged] + [
                functools.partial(exchange, chosen, level_now) for chosen in range(1, every_group + 1)
            ]
            current, acc = lax.switch(pattern[level_now], branches, (current, acc))
        else:
            whole = functools.partial(exchange, every_group, level_now)
            current, acc = lax.cond(pattern[level_now] > 0, whole, unchanged, (current, acc))
    return current[None]


def solution(mesh):
    placed = (
        P(("groups", "space", "blk"), None, None, None),
        P(("groups", "space", "blk"), None, None),
        P(("groups", "space", "blk"), "samp", None),
        P(("groups", "space", "blk"), "samp", None),
        P("groups"),
        P("groups", None),
    )
    return jax.shard_map(
        body,
        mesh=mesh,
        in_specs=placed,
        out_specs=P(("groups", "space", "blk"), "samp", None),
        check_vma=False,
    )
```

```python
import functools

import jax
import jax.numpy as jnp
from jax import lax
from jax.experimental import pallas as pl
from jax.experimental.pallas import tpu as pltpu
from jax.sharding import PartitionSpec as P

LEVELS = 4
REACH = 1


def window_pairs(space_count, part_size, distance, offset):
    pairs = []
    for space_to in range(space_count):
        space_from = space_to + distance
        if not 0 <= space_from < space_count:
            continue
        for blk_to in range(part_size):
            blk_from = (blk_to + offset) % part_size
            pairs.append((space_from * part_size + blk_from, space_to * part_size + blk_to))
    return pairs


def neighbourhood(local_block):
    part_size = lax.axis_size("blk")
    space_count = lax.axis_size("space")
    pieces = []
    for distance in range(-REACH, REACH + 1):
        for offset in range(part_size):
            if distance == 0 and offset == 0:
                pieces.append(local_block)
                continue
            pairs = window_pairs(space_count, part_size, distance, offset)
            pieces.append(lax.ppermute(local_block, ("space", "blk"), pairs))
    return pieces


def step_kernel(n_pieces, neigh, level_now, pick_ref, use_ref, flag_ref, total_hbm, block_hbm, coeff_hbm, solve_hbm, *rest):
    pieces = rest[:n_pieces]
    total_out, block_out, total_v, block_v, values, weights, solve_v, sems, own_sems = rest[n_pieces:]
    take_total = pltpu.make_async_copy(total_hbm, total_v, own_sems.at[0])
    take_total.start()
    for j in range(neigh):

        @pl.when(use_ref[level_now, j] != 0)
        def _():
            pltpu.make_async_copy(coeff_hbm.at[0, j], weights.at[j], sems.at[1, j]).start()

        for p in range(n_pieces):

            @pl.when((pick_ref[j] == p) & (use_ref[level_now, j] != 0))
            def _():
                pltpu.make_async_copy(pieces[p], values.at[j], sems.at[0, j]).start()

    take_solve = pltpu.make_async_copy(solve_hbm.at[0], solve_v, own_sems.at[1])

    @pl.when(flag_ref[level_now] != 0)
    def _():
        take_solve.start()

    take_total.wait()
    for j in range(neigh):

        @pl.when(use_ref[level_now, j] != 0)
        def _():
            pltpu.make_async_copy(pieces[0], values.at[j], sems.at[0, j]).wait()
            pltpu.make_async_copy(coeff_hbm.at[0, j], weights.at[j], sems.at[1, j]).wait()
            total_v[...] -= jnp.dot(values[j], weights[j], preferred_element_type=jnp.float32)

    put_total = pltpu.make_async_copy(total_v, total_out, own_sems.at[3])
    put_total.start()

    @pl.when(flag_ref[level_now] != 0)
    def _():
        take_solve.wait()
        right_side = total_v[...].astype(jnp.bfloat16)
        block_v[...] = jnp.dot(right_side, solve_v[...], preferred_element_type=jnp.float32).astype(block_v.dtype)

        put_block = pltpu.make_async_copy(block_v, block_out, own_sems.at[4])
        put_block.start()
        put_block.wait()

    put_total.wait()


def step(pick, uses, flags, level_now, total, block, coeff, solve, pieces, in_place=True):
    neigh = coeff.shape[1]
    rows, cols = total.shape
    smem = pl.BlockSpec(memory_space=pltpu.SMEM)
    anywhere = pl.BlockSpec(memory_space=pl.ANY)
    return pl.pallas_call(
        functools.partial(step_kernel, len(pieces), neigh, level_now),
        out_shape=(jax.ShapeDtypeStruct((rows, cols), jnp.float32), jax.ShapeDtypeStruct((rows, cols), block.dtype)),
        in_specs=[smem, smem, smem] + [anywhere] * (4 + len(pieces)),
        out_specs=(anywhere, anywhere),
        input_output_aliases={3: 0, 4: 1} if in_place else {},
        scratch_shapes=[
            pltpu.VMEM((rows, cols), jnp.float32),
            pltpu.VMEM((rows, cols), block.dtype),
            pltpu.VMEM((neigh, rows, coeff.shape[2]), pieces[0].dtype),
            pltpu.VMEM(coeff.shape[1:], coeff.dtype),
            pltpu.VMEM(solve.shape[1:], solve.dtype),
            pltpu.SemaphoreType.DMA((2, neigh)),
            pltpu.SemaphoreType.DMA((5,)),
        ],
        cost_estimate=pl.CostEstimate(
            flops=2 * rows * cols * coeff.shape[2] * (neigh + 1),
            bytes_accessed=(2 * neigh + 4) * rows * cols * 4 + coeff.size * 2,
            transcendentals=0,
        ),
    )(pick, uses, flags, total, block, coeff, solve, *pieces)


def plan_kernel(count, neigh, part_size, groups, owner_ref, nbrs_ref, where_ref, pick_ref, use_ref, flag_ref, need_ref, levels):
    space_index, blk_index = where_ref[0], where_ref[1]
    own_slot = space_index * part_size + blk_index
    for b in range(count):
        levels[b] = 0

    def sweep(step_index, carry):
        def one_block(b, carry):
            deepest = jnp.int32(0)
            for j in range(neigh):
                listed = nbrs_ref[b, j]
                later = jnp.where(listed >= count, levels[jnp.remainder(listed, count)] + 1, 0)
                deepest = jnp.maximum(deepest, later)
            levels[b] = deepest
            return carry

        return lax.fori_loop(0, count, one_block, carry)

    lax.fori_loop(0, LEVELS, sweep, 0)

    def find(b, found):
        return jnp.where(owner_ref[b] == own_slot, b, found)

    own_block = lax.fori_loop(0, count, find, jnp.int32(0))
    own_level = levels[own_block]
    for r in range(LEVELS):
        flag_ref[r] = (own_level == r).astype(jnp.int32)
        for g in range(groups):
            need_ref[r, g] = 0
    for j in range(neigh):
        listed = nbrs_ref[own_block, j]
        target = jnp.remainder(listed, count)
        near = owner_ref[target]
        distance = near // part_size - space_index + REACH
        offset = jnp.remainder(jnp.remainder(near, part_size) - blk_index + part_size, part_size)
        pick_ref[j] = distance * part_size + offset
        arrives = jnp.where(listed >= count, levels[target] + 1, 0)
        for r in range(LEVELS):
            use_ref[r, j] = (arrives == r).astype(jnp.int32)

    def mark(b, carry):
        slot = owner_ref[b]
        for j in range(neigh):
            listed = nbrs_ref[b, j]
            target = jnp.remainder(listed, count)
            near = owner_ref[target]
            arrives = levels[target] + 1
            group = near // part_size - slot // part_size + REACH
            fine = (listed >= count) & (near != slot) & (arrives < LEVELS) & (group >= 0) & (group < groups)

            @pl.when(fine)
            def _():
                need_ref[arrives, group] = 1

        return carry

    lax.fori_loop(0, count, mark, 0)


def plan(owner, nbrs, where, part_size):
    count, neigh = nbrs.shape
    groups = 2 * REACH + 1
    smem = pl.BlockSpec(memory_space=pltpu.SMEM)
    return pl.pallas_call(
        functools.partial(plan_kernel, count, neigh, part_size, groups),
        out_shape=(
            jax.ShapeDtypeStruct((neigh,), jnp.int32),
            jax.ShapeDtypeStruct((LEVELS, neigh), jnp.int32),
            jax.ShapeDtypeStruct((LEVELS,), jnp.int32),
            jax.ShapeDtypeStruct((LEVELS, groups), jnp.int32),
        ),
        in_specs=[smem, smem, smem],
        out_specs=(smem, smem, smem, smem),
        scratch_shapes=[pltpu.SMEM((count,), jnp.int32)],
    )(owner, nbrs, where)


def body(coeff, solve, noise, prior, owner, nbrs):
    part_size = lax.axis_size("blk")
    space_index = lax.axis_index("space")
    blk_index = lax.axis_index("blk")
    where = jnp.stack([space_index, blk_index]).astype(jnp.int32)
    pick, uses, flags, need = plan(owner, nbrs, where, part_size)
    groups = jnp.arange(2 * REACH + 1, dtype=jnp.int32)
    if lax.axis_size("groups") == 2:
        need = jnp.maximum(need, lax.ppermute(need, "groups", [(0, 1), (1, 0)]))
    else:
        need = lax.pmax(need, "groups")
    pattern = jnp.sum(need * (2 ** groups)[None, :], axis=1)

    prior_pieces = neighbourhood(prior[0])

    def unchanged(previous):
        return previous

    def finished(block, total):
        right_side = total.astype(jnp.bfloat16)
        return jnp.dot(right_side, solve[0], preferred_element_type=jnp.float32).astype(jnp.bfloat16)

    def exchange(chosen, level_now, carry):
        block, total = carry
        space_count = lax.axis_size("space")
        pieces = []
        for distance in range(-REACH, REACH + 1):
            for offset in range(part_size):
                if (distance == 0 and offset == 0) or not chosen & (1 << (distance + REACH)):
                    pieces.append(prior_pieces[len(pieces)])
                    continue
                pairs = window_pairs(space_count, part_size, distance, offset)
                pieces.append(lax.ppermute(block, ("space", "blk"), pairs))
        total, block = step(pick, uses, flags, level_now, total, block, coeff, solve, pieces)
        return block, total

    acc, current = step(pick, uses, flags, 0, noise[0], prior[0], coeff, solve, prior_pieces, in_place=False)
    every_group = 2 ** (2 * REACH + 1) - 1
    for level_now in range(1, LEVELS):
        if level_now == 2:
            branches = [unchanged] + [
                functools.partial(exchange, chosen, level_now) for chosen in range(1, every_group + 1)
            ]
            current, acc = lax.switch(pattern[level_now], branches, (current, acc))
        else:
            whole = functools.partial(exchange, every_group, level_now)
            current, acc = lax.cond(pattern[level_now] > 0, whole, unchanged, (current, acc))
    return current[None]


def solution(mesh):
    placed = (
        P(("groups", "space", "blk"), None, None, None),
        P(("groups", "space", "blk"), None, None),
        P(("groups", "space", "blk"), "samp", None),
        P(("groups", "space", "blk"), "samp", None),
        P("groups"),
        P("groups", None),
    )
    return jax.shard_map(
        body,
        mesh=mesh,
        in_specs=placed,
        out_specs=P(("groups", "space", "blk"), "samp", None),
        check_vma=False,
    )
```

```python
import functools

import jax
import jax.numpy as jnp
from jax import lax
from jax.experimental import pallas as pl
from jax.experimental.pallas import tpu as pltpu
from jax.sharding import PartitionSpec as P

LEVELS = 4
REACH = 1


def window_pairs(space_count, part_size, distance, offset):
    pairs = []
    for space_to in range(space_count):
        space_from = space_to + distance
        if not 0 <= space_from < space_count:
            continue
        for blk_to in range(part_size):
            blk_from = (blk_to + offset) % part_size
            pairs.append((space_from * part_size + blk_from, space_to * part_size + blk_to))
    return pairs


def neighbourhood(local_block):
    part_size = lax.axis_size("blk")
    space_count = lax.axis_size("space")
    pieces = []
    for distance in range(-REACH, REACH + 1):
        for offset in range(part_size):
            if distance == 0 and offset == 0:
                pieces.append(local_block)
                continue
            pairs = window_pairs(space_count, part_size, distance, offset)
            pieces.append(lax.ppermute(local_block, ("space", "blk"), pairs))
    return pieces


def step_kernel(n_pieces, neigh, level_now, pick_ref, use_ref, flag_ref, total_hbm, block_hbm, coeff_hbm, solve_hbm, *rest):
    pieces = rest[:n_pieces]
    total_out, block_out, total_v, block_v, values, weights, solve_v, sems, own_sems = rest[n_pieces:]
    take_total = pltpu.make_async_copy(total_hbm, total_v, own_sems.at[0])
    take_total.start()
    for j in range(neigh):

        @pl.when(use_ref[level_now, j] != 0)
        def _():
            pltpu.make_async_copy(coeff_hbm.at[0, j], weights.at[j], sems.at[1, j]).start()

        for p in range(n_pieces):

            @pl.when((pick_ref[j] == p) & (use_ref[level_now, j] != 0))
            def _():
                pltpu.make_async_copy(pieces[p], values.at[j], sems.at[0, j]).start()

    take_solve = pltpu.make_async_copy(solve_hbm.at[0], solve_v, own_sems.at[1])

    @pl.when(flag_ref[level_now] != 0)
    def _():
        take_solve.start()

    take_total.wait()
    for j in range(neigh):

        @pl.when(use_ref[level_now, j] != 0)
        def _():
            pltpu.make_async_copy(pieces[0], values.at[j], sems.at[0, j]).wait()
            pltpu.make_async_copy(coeff_hbm.at[0, j], weights.at[j], sems.at[1, j]).wait()
            total_v[...] -= jnp.dot(values[j], weights[j], preferred_element_type=jnp.float32)

    put_total = pltpu.make_async_copy(total_v, total_out, own_sems.at[3])
    put_total.start()

    @pl.when(flag_ref[level_now] != 0)
    def _():
        take_solve.wait()
        right_side = total_v[...].astype(jnp.bfloat16)
        block_v[...] = jnp.dot(right_side, solve_v[...], preferred_element_type=jnp.float32).astype(block_v.dtype)

        put_block = pltpu.make_async_copy(block_v, block_out, own_sems.at[4])
        put_block.start()
        put_block.wait()

    put_total.wait()


def step(pick, uses, flags, level_now, total, block, coeff, solve, pieces, in_place=True):
    neigh = coeff.shape[1]
    rows, cols = total.shape
    smem = pl.BlockSpec(memory_space=pltpu.SMEM)
    anywhere = pl.BlockSpec(memory_space=pl.ANY)
    return pl.pallas_call(
        functools.partial(step_kernel, len(pieces), neigh, level_now),
        out_shape=(jax.ShapeDtypeStruct((rows, cols), jnp.float32), jax.ShapeDtypeStruct((rows, cols), block.dtype)),
        in_specs=[smem, smem, smem] + [anywhere] * (4 + len(pieces)),
        out_specs=(anywhere, anywhere),
        input_output_aliases={3: 0, 4: 1} if in_place else {},
        scratch_shapes=[
            pltpu.VMEM((rows, cols), jnp.float32),
            pltpu.VMEM((rows, cols), block.dtype),
            pltpu.VMEM((neigh, rows, coeff.shape[2]), pieces[0].dtype),
            pltpu.VMEM(coeff.shape[1:], coeff.dtype),
            pltpu.VMEM(solve.shape[1:], solve.dtype),
            pltpu.SemaphoreType.DMA((2, neigh)),
            pltpu.SemaphoreType.DMA((5,)),
        ],
        cost_estimate=pl.CostEstimate(
            flops=2 * rows * cols * coeff.shape[2] * (neigh + 1),
            bytes_accessed=(2 * neigh + 4) * rows * cols * 4 + coeff.size * 2,
            transcendentals=0,
        ),
    )(pick, uses, flags, total, block, coeff, solve, *pieces)


def plan_kernel(count, neigh, part_size, groups, owner_ref, nbrs_ref, pick_ref, use_ref, flag_ref, need_ref, levels):
    space_index, blk_index = lax.axis_index("space"), lax.axis_index("blk")
    unroll = count <= 16
    own_slot = space_index * part_size + blk_index
    for b in range(count):
        levels[b] = 0

    def sweep(step_index, carry):
        def one_block(b, carry):
            deepest = jnp.int32(0)
            for j in range(neigh):
                listed = nbrs_ref[b, j]
                later = jnp.where(listed >= count, levels[jnp.remainder(listed, count)] + 1, 0)
                deepest = jnp.maximum(deepest, later)
            levels[b] = deepest
            return carry

        return lax.fori_loop(0, count, one_block, carry, unroll=unroll)

    lax.fori_loop(0, LEVELS, sweep, 0)

    def find(b, found):
        return jnp.where(owner_ref[b] == own_slot, b, found)

    own_block = lax.fori_loop(0, count, find, jnp.int32(0), unroll=unroll)
    own_level = levels[own_block]
    for r in range(LEVELS):
        flag_ref[r] = (own_level == r).astype(jnp.int32)
        for g in range(groups):
            need_ref[r, g] = 0
    for j in range(neigh):
        listed = nbrs_ref[own_block, j]
        target = jnp.remainder(listed, count)
        near = owner_ref[target]
        distance = near // part_size - space_index + REACH
        offset = jnp.remainder(jnp.remainder(near, part_size) - blk_index + part_size, part_size)
        pick_ref[j] = distance * part_size + offset
        arrives = jnp.where(listed >= count, levels[target] + 1, 0)
        for r in range(LEVELS):
            use_ref[r, j] = (arrives == r).astype(jnp.int32)

    def mark(b, carry):
        slot = owner_ref[b]
        for j in range(neigh):
            listed = nbrs_ref[b, j]
            target = jnp.remainder(listed, count)
            near = owner_ref[target]
            arrives = levels[target] + 1
            group = near // part_size - slot // part_size + REACH
            fine = (listed >= count) & (near != slot) & (arrives < LEVELS) & (group >= 0) & (group < groups)

            @pl.when(fine)
            def _():
                need_ref[arrives, group] = 1

        return carry

    lax.fori_loop(0, count, mark, 0, unroll=unroll)


def plan(owner, nbrs, part_size):
    count, neigh = nbrs.shape
    groups = 2 * REACH + 1
    smem = pl.BlockSpec(memory_space=pltpu.SMEM)
    return pl.pallas_call(
        functools.partial(plan_kernel, count, neigh, part_size, groups),
        out_shape=(
            jax.ShapeDtypeStruct((neigh,), jnp.int32),
            jax.ShapeDtypeStruct((LEVELS, neigh), jnp.int32),
            jax.ShapeDtypeStruct((LEVELS,), jnp.int32),
            jax.ShapeDtypeStruct((LEVELS, groups), jnp.int32),
        ),
        in_specs=[smem, smem],
        out_specs=(smem, smem, smem, smem),
        scratch_shapes=[pltpu.SMEM((count,), jnp.int32)],
    )(owner, nbrs)


def body(coeff, solve, noise, prior, owner, nbrs):
    part_size = lax.axis_size("blk")
    space_index = lax.axis_index("space")
    blk_index = lax.axis_index("blk")
    pick, uses, flags, need = plan(owner, nbrs, part_size)
    groups = jnp.arange(2 * REACH + 1, dtype=jnp.int32)
    if lax.axis_size("groups") == 2:
        need = jnp.maximum(need, lax.ppermute(need, "groups", [(0, 1), (1, 0)]))
    else:
        need = lax.pmax(need, "groups")
    pattern = jnp.sum(need * (2 ** groups)[None, :], axis=1)

    prior_pieces = neighbourhood(prior[0])

    def unchanged(previous):
        return previous

    def finished(block, total):
        right_side = total.astype(jnp.bfloat16)
        return jnp.dot(right_side, solve[0], preferred_element_type=jnp.float32).astype(jnp.bfloat16)

    def exchange(chosen, level_now, carry):
        block, total = carry
        space_count = lax.axis_size("space")
        pieces = []
        for distance in range(-REACH, REACH + 1):
            for offset in range(part_size):
                if (distance == 0 and offset == 0) or not chosen & (1 << (distance + REACH)):
                    pieces.append(prior_pieces[len(pieces)])
                    continue
                pairs = window_pairs(space_count, part_size, distance, offset)
                pieces.append(lax.ppermute(block, ("space", "blk"), pairs))
        total, block = step(pick, uses, flags, level_now, total, block, coeff, solve, pieces)
        return block, total

    acc, current = step(pick, uses, flags, 0, noise[0], prior[0], coeff, solve, prior_pieces, in_place=False)
    every_group = 2 ** (2 * REACH + 1) - 1
    for level_now in range(1, LEVELS):
        if level_now == 2:
            branches = [unchanged] + [
                functools.partial(exchange, chosen, level_now) for chosen in range(1, every_group + 1)
            ]
            current, acc = lax.switch(pattern[level_now], branches, (current, acc))
        else:
            whole = functools.partial(exchange, every_group, level_now)
            current, acc = lax.cond(pattern[level_now] > 0, whole, unchanged, (current, acc))
    return current[None]


def solution(mesh):
    placed = (
        P(("groups", "space", "blk"), None, None, None),
        P(("groups", "space", "blk"), None, None),
        P(("groups", "space", "blk"), "samp", None),
        P(("groups", "space", "blk"), "samp", None),
        P("groups"),
        P("groups", None),
    )
    return jax.shard_map(
        body,
        mesh=mesh,
        in_specs=placed,
        out_specs=P(("groups", "space", "blk"), "samp", None),
        check_vma=False,
    )
```
